512 devices in a mesh: ctx: 16 (over z), ep: 32 (over y, x, core).
Axes of the slice: x: 4, y: 4, z: 16, core: 2. Of those that a mesh axis runs over, the one named last changes fastest.
Arguments:
- query_act: bfloat16 [2048, 8192], P('ctx', 'ep'), may hold values from -6 to 6
- key_act: bfloat16 [2048, 8192], P('ctx', 'ep'), may hold values from -6 to 6
- value_act: bfloat16 [2048, 8192], P('ctx', 'ep'), may hold values from -6 to 6
- state_init: float32 [64, 128, 128], P('ep'), may hold values from -128 to 128
- head_gain: float32 [8192], P('ep'), may hold values from 0.25 to 1.75
- out_weight: bfloat16 [8192, 3072], P('ctx', 'ep'), may hold values from -0.0625 to 0.0625
- stream_in: bfloat16 [2048, 3072], P('ctx', 'ep'), may hold values from -150 to 150
- model_gain: float32 [3072], replicated, may hold values from 0.25 to 1.75
- expert_ids: int32 [2048, 2], P('ctx'), may hold values from 0 to 15, as said below
- expert_slots: int32 [2048, 2], P('ctx'), may hold values from 0 to 19, as said below
- route_gates: float32 [2048, 2], P('ctx'), may hold values from 0.2 to 1
- gate_weight: bfloat16 [32, 3072, 3072], P('ep', 'ctx'), may hold values from -0.109375 to 0.109375
- up_weight: bfloat16 [32, 3072, 3072], P('ep', 'ctx'), may hold values from -0.109375 to 0.109375
- down_weight: bfloat16 [32, 3072, 3072], P('ep', 'ctx'), may hold values from -0.078125 to 0.078125
- out_grad: bfloat16 [2048, 3072], P('ctx', 'ep'), may hold values from -6 to 6
Outputs:
- layer_out: bfloat16 [2048, 3072], P('ctx', 'ep')
- grad_query: bfloat16 [2048, 8192], P('ctx', 'ep')
- grad_key: bfloat16 [2048, 8192], P('ctx', 'ep')
- grad_value: bfloat16 [2048, 8192], P('ctx', 'ep')
- grad_state: float32 [64, 128, 128], P('ep')
- grad_stream: bfloat16 [2048, 3072], P('ctx', 'ep')
The draws below stay inside these ranges and needn't reach their ends.
Inputs may be any that keep to these rules, and one draw needn't show every extreme that they name: `expert_ids`: within each block of 128 tokens a token's two experts differ; the tokens naming expert e hold the slots 0 to n - 1 of e once each, n being their number; no expert is named by more than 20 tokens of a block, and in every block some expert by exactly 20. `expert_slots`: see expert_ids.
All inputs are finite; a program needn't handle non-finite values.
Results may differ from the reference program's by a relative error of at most 0.02.
Values may be sent and summed in bfloat16 or wider, within the bound.
No kernel may reach another device: no remote copies, remote signals or barrier semaphores. Data moves between devices by JAX's collectives and lax.ppermute only.
A program may use at most 64 MiB of HBM per device.

```python
import math
import jax
import jax.numpy as jnp
from jax import lax

D = 3072
HD = 128
EXPERT_FF = 6144
TOK_CTX = 128
HEADS = 64
EXPERTS = 16
TOKENS = 2048
C_CH = 20
SLOTS = 320
HBLOCK = 192


def route_tables(key):
    base = jax.random.fold_in(key, 17)
    blocks = TOKENS // TOK_CTX
    tokens_here = TOK_CTX
    remaining = 2 * tokens_here - C_CH
    others = EXPERTS - 1
    common = remaining // others
    extra = remaining % others
    spread = max(1, min(common, C_CH - common - 1))

    def one_block(block_key):
        key_order, key_shift, key_perm, key_swap = jax.random.split(block_key, 4)
        order = jax.random.permutation(key_order, EXPERTS)
        shifts = jax.random.randint(key_shift, (others,), 0, spread)
        moved = shifts - jnp.roll(shifts, -1)
        ranked = jnp.concatenate([jnp.full((1,), C_CH, jnp.int32), (common + (jnp.arange(others) < extra) + moved).astype(jnp.int32)])
        counts = jnp.zeros((EXPERTS,), jnp.int32).at[order].set(ranked)
        ends = jnp.cumsum(counts)
        starts = ends - counts
        places = jnp.arange(2 * tokens_here, dtype=jnp.int32)
        labels = jnp.sum((ends[None, :] <= places[:, None]).astype(jnp.int32), 1)
        owned = labels[:, None] == jnp.arange(EXPERTS)[None, :]
        slot_of = places - jnp.sum(jnp.where(owned, starts[None, :], 0), 1)
        pair_ids = jnp.stack([labels[:tokens_here], labels[tokens_here:]], -1)
        pair_slots = jnp.stack([slot_of[:tokens_here], slot_of[tokens_here:]], -1)
        shuffle = jax.random.permutation(key_perm, tokens_here)
        pair_ids = pair_ids[shuffle]
        pair_slots = pair_slots[shuffle]
        flips = jax.random.randint(key_swap, (tokens_here, 1), 0, 2) == 1
        pair_ids = jnp.where(flips, pair_ids[:, ::-1], pair_ids)
        pair_slots = jnp.where(flips, pair_slots[:, ::-1], pair_slots)
        return (pair_ids.astype(jnp.int32), pair_slots.astype(jnp.int32))
    block_keys = jax.vmap(lambda index: jax.random.fold_in(base, index))(jnp.arange(blocks))
    all_ids, all_slots = jax.vmap(one_block)(block_keys)
    return (all_ids.reshape(TOKENS, 2), all_slots.reshape(TOKENS, 2))


def draw_expert_ids(key, part):
    return route_tables(key)[0]


def draw_expert_slots(key, part):
    return route_tables(key)[1]


def draw_stream_in(key, part):
    key_cols, key_rows, key_vals = jax.random.split(key, 3)
    rising = 1.0 + 2.0 * jnp.arange(D, dtype=jnp.float32)[None, :] / D
    column_scale = jnp.exp(jax.random.uniform(key_cols, (1, D)) * math.log(10.0)) * rising
    row_scale = jnp.exp(jax.random.uniform(key_rows, (TOKENS, 1)) * math.log(4.0))
    values = jnp.clip(jax.random.normal(key_vals, (TOKENS, D)), -6.0, 6.0)
    return (0.12 * values * row_scale * column_scale).astype(jnp.bfloat16)


def level_of(rng, dims, cuts, smallest, high):
    def one(axis_at, parts):
        draws = jax.random.uniform(jax.random.fold_in(jax.random.fold_in(rng, 6), axis_at), (parts,), jnp.float32, smallest / len(cuts), high / len(cuts))
        return jnp.repeat(jnp.exp(draws), dims[axis_at] // parts).reshape((-1,) + (1,) * (len(dims) - axis_at - 1))

    level = one(*cuts[0])
    for cut in cuts[1:]:
        level = level * one(*cut)
    return level


def normal_values(key, dims, width, bound, shards=(), kind=jnp.bfloat16):
    result = width * jax.random.normal(key, dims, jnp.float32)
    if shards:
        result = result * level_of(key, dims, shards, -0.22, 0.18)
    return jnp.clip(result, -bound, bound).astype(kind)


def setup_inputs(seed: int = 0) -> dict:
    key_list = jax.random.split(jax.random.key(seed), 16)
    query_act = normal_values(key_list[0], (TOKENS, HEADS * HD), 1.0, 6.0, ((0, 16), (1, 32)))
    key_act = normal_values(key_list[1], (TOKENS, HEADS * HD), 1.0, 6.0, ((0, 16), (1, 32)))
    value_act = normal_values(key_list[2], (TOKENS, HEADS * HD), 1.0, 6.0, ((0, 16), (1, 32)))
    state_init = normal_values(key_list[3], (HEADS, HD, HD), 20.0, 128.0, ((0, 32),), jnp.float32)
    head_gain = jnp.clip(1.0 + 0.15 * jax.random.normal(key_list[4], (HEADS * HD,), jnp.float32), 0.25, 1.75)
    out_weight = normal_values(key_list[5], (HEADS * HD, D), (HEADS * HD) ** -0.5, 0.0625, ((0, 16), (1, 32)))
    stream_in = draw_stream_in(jax.random.fold_in(key_list[15], 71), 0)
    model_gain = jnp.clip(1.0 + 0.15 * jax.random.normal(key_list[7], (D,), jnp.float32), 0.25, 1.75)
    expert_ids = draw_expert_ids(jax.random.fold_in(key_list[15], 71), 0)
    expert_slots = draw_expert_slots(jax.random.fold_in(key_list[15], 71), 0)
    route_gates = jnp.clip(0.2 + 0.8 * jax.random.uniform(key_list[10], (TOKENS, 2), jnp.float32) ** level_of(key_list[10], (TOKENS, 2), ((0, 16),), -0.2, 0.2), 0.2, 1.0)
    gate_weight = normal_values(key_list[11], (2 * EXPERTS, EXPERT_FF // 2, D), D ** -0.5, 0.109375, ((0, 32), (1, 16)))
    up_weight = normal_values(key_list[12], (2 * EXPERTS, EXPERT_FF // 2, D), D ** -0.5, 0.109375, ((0, 32), (1, 16)))
    down_weight = normal_values(key_list[13], (2 * EXPERTS, EXPERT_FF // 2, D), EXPERT_FF ** -0.5, 0.078125, ((0, 32), (1, 16)))
    out_grad = normal_values(key_list[14], (TOKENS, D), 1.0, 6.0, ((0, 16), (1, 32)))
    return {"query_act": query_act, "key_act": key_act, "value_act": value_act, "state_init": state_init, "head_gain": head_gain, "out_weight": out_weight, "stream_in": stream_in, "model_gain": model_gain, "expert_ids": expert_ids, "expert_slots": expert_slots, "route_gates": route_gates, "gate_weight": gate_weight, "up_weight": up_weight, "down_weight": down_weight, "out_grad": out_grad}


def head_normalize(attended, gain):
    factor = lax.rsqrt(lax.optimization_barrier(jnp.mean(attended * attended, -1, keepdims=True)) + 1e-06)
    return attended * factor * gain

def model_normalize(stream_f, model_gain):
    factor = lax.rsqrt(lax.optimization_barrier(jnp.mean(stream_f * stream_f, -1, keepdims=True)) + 1e-05)
    return stream_f * factor * model_gain

def round_bf(value):
    return lax.optimization_barrier(value.astype(jnp.bfloat16)).astype(jnp.float32)

def reference(query_act, key_act, value_act, state_init, head_gain, out_weight, stream_in, model_gain, expert_ids, expert_slots, route_gates, gate_weight, up_weight, down_weight, out_grad):
    f32 = jnp.float32
    high = lax.Precision.HIGHEST
    blocks = TOKENS // TOK_CTX
    query4 = query_act.astype(f32).reshape(blocks, TOK_CTX, HEADS, HD)
    key4 = key_act.astype(f32).reshape(blocks, TOK_CTX, HEADS, HD)
    value4 = value_act.astype(f32).reshape(blocks, TOK_CTX, HEADS, HD)
    kv_blocks = jnp.einsum('cthd,cthe->chde', key4, value4)
    running = jnp.cumsum(kv_blocks, 0)
    before = jnp.concatenate([jnp.zeros_like(kv_blocks[:1]), running[:-1]], 0)
    prefix = state_init[None] + before
    causal = jnp.arange(TOK_CTX)[:, None] >= jnp.arange(TOK_CTX)[None, :]
    scores = jnp.einsum('cthd,cshd->chts', query4, key4)
    scores_bf = jnp.where(causal[None, None], scores, 0.0).astype(jnp.bfloat16)
    inside = jnp.einsum('chts,cshe->cthe', scores_bf.astype(f32), value4)
    from_state = jnp.einsum('cthd,chde->cthe', query4, prefix, precision=high)
    attended = from_state + inside
    gain_heads = head_gain.reshape(HEADS, HD)
    normed_heads = head_normalize(attended, gain_heads).astype(jnp.bfloat16).reshape(TOKENS, HEADS * HD)
    stream = (stream_in.astype(f32) + jnp.dot(normed_heads, out_weight, preferred_element_type=f32)).astype(jnp.bfloat16)
    stream_f = stream.astype(f32)
    model_in = model_normalize(stream_f, model_gain).astype(jnp.bfloat16)
    block_of = (jnp.arange(TOKENS) // TOK_CTX).astype(jnp.int32)
    slot_row = block_of[:, None] * C_CH + expert_slots
    spread_in = jnp.broadcast_to(model_in[:, None, :], (TOKENS, 2, D))
    slot_in = jnp.zeros((EXPERTS, SLOTS, D), jnp.bfloat16).at[expert_ids, slot_row].set(spread_in)
    half_units = EXPERT_FF // 2
    saved = []
    outputs = []
    for expert in range(EXPERTS):
        w_gate = jnp.concatenate([gate_weight[expert], gate_weight[expert + EXPERTS]], 0).T
        w_up = jnp.concatenate([up_weight[expert], up_weight[expert + EXPERTS]], 0).T
        w_down = jnp.concatenate([down_weight[expert], down_weight[expert + EXPERTS]], 0)
        pre_gate = jnp.dot(slot_in[expert], w_gate, preferred_element_type=f32)
        pre_up = jnp.dot(slot_in[expert], w_up, preferred_element_type=f32)
        activated = (jax.nn.silu(pre_gate) * pre_up).astype(jnp.bfloat16)
        halves = []
        for half in range(2):
            summed = jnp.zeros((SLOTS, D), f32)
            for index in range(half_units // HBLOCK):
                lower = half * half_units + index * HBLOCK
                term = jnp.dot(activated[:, lower:lower + HBLOCK], w_down[lower:lower + HBLOCK], preferred_element_type=f32)
                summed = summed + round_bf(term)
            halves.append(summed.astype(jnp.bfloat16).astype(f32))
        outputs.append(halves[0] + halves[1])
        saved.append((w_gate, w_up, w_down, pre_gate, pre_up))
    expert_out = jnp.stack(outputs, 0)
    expert_mix = lax.optimization_barrier(jnp.sum(route_gates[:, :, None] * expert_out[expert_ids, slot_row], 1))
    layer_out = (stream_f + expert_mix).astype(jnp.bfloat16)
    grad_out = out_grad.astype(f32)
    gated = (route_gates[:, :, None] * grad_out[:, None, :]).astype(jnp.bfloat16)
    grad_rows = jnp.zeros((EXPERTS, SLOTS, D), jnp.bfloat16).at[expert_ids, slot_row].set(gated)
    back = []
    for expert in range(EXPERTS):
        w_gate, w_up, w_down, pre_gate, pre_up = saved[expert]
        grad_act = jnp.dot(grad_rows[expert], w_down.T, preferred_element_type=f32)
        gate_sig = jax.nn.sigmoid(pre_gate)
        grad_gate_pre = (grad_act * pre_up * gate_sig * (1.0 + pre_gate * (1.0 - gate_sig))).astype(jnp.bfloat16)
        grad_up_pre = (grad_act * pre_gate * gate_sig).astype(jnp.bfloat16)
        halves = []
        for half in range(2):
            summed = jnp.zeros((SLOTS, D), f32)
            for index in range(half_units // HBLOCK):
                lower = half * half_units + index * HBLOCK
                term = jnp.dot(grad_gate_pre[:, lower:lower + HBLOCK], w_gate[:, lower:lower + HBLOCK].T, preferred_element_type=f32)
                term = term + jnp.dot(grad_up_pre[:, lower:lower + HBLOCK], w_up[:, lower:lower + HBLOCK].T, preferred_element_type=f32)
                summed = summed + round_bf(term)
            halves.append(summed.astype(jnp.bfloat16).astype(f32))
        back.append(halves[0] + halves[1])
    grad_slots_all = jnp.stack(back, 0)
    grad_model_in = lax.optimization_barrier(jnp.sum(grad_slots_all[expert_ids, slot_row], 1))
    norm_pull = jax.vjp(lambda value: model_normalize(value, model_gain), stream_f)[1]
    grad_stream = (grad_out + norm_pull(grad_model_in)[0]).astype(jnp.bfloat16)
    grad_heads = jnp.dot(grad_stream, out_weight.T, preferred_element_type=f32).reshape(blocks, TOK_CTX, HEADS, HD)
    head_pull = jax.vjp(lambda value: head_normalize(value, gain_heads), attended)[1]
    grad_attended = head_pull(grad_heads)[0].astype(jnp.bfloat16).astype(f32)
    state_part = jnp.einsum('cthd,cthe->chde', query4, grad_attended)
    reverse_run = jnp.cumsum(state_part[::-1], 0)[::-1]
    later = jnp.concatenate([reverse_run[1:], jnp.zeros_like(state_part[:1])], 0)
    grad_state = lax.optimization_barrier(jnp.sum(state_part, 0))
    grad_scores = jnp.einsum('cthe,cshe->chts', grad_attended, value4)
    grad_masked = jnp.where(causal[None, None], grad_scores, 0.0).astype(jnp.bfloat16).astype(f32)
    grad_query = jnp.einsum('cthe,chde->cthd', grad_attended, prefix, precision=high) + jnp.einsum('chts,cshd->cthd', grad_masked, key4)
    grad_key = jnp.einsum('cthe,chde->cthd', value4, later, precision=high) + jnp.einsum('chts,cthd->cshd', grad_masked, query4)
    grad_value = jnp.einsum('cthd,chde->cthe', key4, later, precision=high) + jnp.einsum('chts,cthe->cshe', scores_bf.astype(f32), grad_attended)
    shape_out = (TOKENS, HEADS * HD)
    return (layer_out, grad_query.astype(jnp.bfloat16).reshape(shape_out), grad_key.astype(jnp.bfloat16).reshape(shape_out), grad_value.astype(jnp.bfloat16).reshape(shape_out), grad_state, grad_stream)
```

```python
import jax
import jax.numpy as jnp
from jax import lax
from jax.sharding import PartitionSpec as P


def butterfly_sums(value, axis, backward):
    count = lax.axis_size(axis)
    place = lax.axis_index(axis)
    total = value
    carried = jnp.zeros_like(value)
    step = 1
    while step < count:
        other = lax.ppermute(total, axis, [(i, i ^ step) for i in range(count)])
        upper = (place & step) != 0
        take = jnp.logical_not(upper) if backward else upper
        carried = carried + jnp.where(take, other, jnp.zeros_like(other))
        total = total + other
        step *= 2
    return carried, total


def gather_blocks(value, axis):
    count = lax.axis_size(axis)
    spread = jnp.broadcast_to(value[None], (count,) + value.shape)
    return lax.all_to_all(spread, axis, 0, 0, tiled=True)


def head_normalize(attended, gain):
    factor = lax.rsqrt(jnp.mean(attended * attended, -1, keepdims=True) + 1e-06)
    return attended * factor * gain


def contract_last(left, right):
    return lax.dot_general(
        left, right, (((1,), (1,)), ((), ())), preferred_element_type=jnp.float32
    )


def local(
    query_act,
    key_act,
    value_act,
    state_init,
    head_gain,
    out_weight,
    stream_in,
    model_gain,
    expert_ids,
    expert_slots,
    route_gates,
    gate_weight,
    up_weight,
    down_weight,
    out_grad,
):
    f32 = jnp.float32
    high = lax.Precision.HIGHEST
    ep_count = lax.axis_size("ep")
    expert_count = ep_count // 2
    my_ep = lax.axis_index("ep")
    tokens_here = query_act.shape[0]
    head_count = state_init.shape[0]
    head_size = state_init.shape[1]
    model_width = model_gain.shape[0]
    columns = stream_in.shape[1]
    capacity = 5 * tokens_here // (2 * expert_count)
    w_cols = lax.all_gather(out_weight, "ctx", axis=0, tiled=True)
    query3 = query_act.reshape(tokens_here, head_count, head_size)
    key3 = key_act.reshape(tokens_here, head_count, head_size)
    value3 = value_act.reshape(tokens_here, head_count, head_size)
    kv_own = jnp.einsum("thd,the->hde", key3, value3, preferred_element_type=f32)
    before, _ = butterfly_sums(kv_own, "ctx", False)
    prefix = state_init + before
    causal = jnp.arange(tokens_here)[:, None] >= jnp.arange(tokens_here)[None, :]
    scores = jnp.einsum("thd,shd->hts", query3, key3, preferred_element_type=f32)
    scores_bf = jnp.where(causal[None], scores, 0.0).astype(jnp.bfloat16)
    inside = jnp.einsum("hts,she->the", scores_bf, value3, preferred_element_type=f32)
    from_state = jnp.einsum("thd,hde->the", query3.astype(f32), prefix, precision=high)
    attended = from_state + inside
    gain_heads = head_gain.reshape(head_count, head_size)
    normed_heads = (
        head_normalize(attended, gain_heads)
        .astype(jnp.bfloat16)
        .reshape(tokens_here, head_count * head_size)
    )
    w_blocks = w_cols.reshape(ep_count, head_count * head_size, columns)
    attn_proj = jnp.einsum(
        "ith,ihf->tf", gather_blocks(normed_heads, "ep"), w_blocks, preferred_element_type=f32
    )
    stream = (stream_in.astype(f32) + attn_proj).astype(jnp.bfloat16)
    stream_f = stream.astype(f32)
    gain_cols = lax.dynamic_slice_in_dim(model_gain, my_ep * columns, columns, 0)
    dest_expert = jnp.arange(ep_count) % expert_count
    slot_iota = jnp.arange(capacity)
    hits = (expert_ids[:, :, None, None] == dest_expert[None, None, :, None]) & (
        expert_slots[:, :, None, None] == slot_iota[None, None, None, :]
    )
    hits_f = hits.astype(f32)
    dest_picks = jnp.sum(hits_f, 1).reshape(tokens_here, ep_count * capacity)
    dest_weights = jnp.sum(hits_f * route_gates[:, :, None, None], 1).reshape(
        tokens_here, ep_count * capacity
    )
    picked = jnp.dot(
        dest_picks.T.astype(jnp.bfloat16), stream, preferred_element_type=f32
    ).astype(jnp.bfloat16)
    arrived = lax.all_to_all(
        picked.reshape(ep_count, capacity, columns), "ep", 0, 0, tiled=True
    )
    slot_rows = arrived.transpose(1, 0, 2).reshape(capacity, model_width).astype(f32)
    slot_scale = lax.rsqrt(jnp.mean(slot_rows * slot_rows, -1, keepdims=True) + 1e-05)
    expert_in = (slot_rows * slot_scale * model_gain).astype(jnp.bfloat16)
    w_gate = gate_weight[0]
    w_up = up_weight[0]
    w_down = down_weight[0]
    hidden_block = w_gate.shape[0]
    w_rows = lax.all_to_all(w_blocks, "ep", 0, 0, tiled=True)
    portion = lax.all_gather(expert_in, "ctx", axis=0, tiled=True)
    portion, w_rows = lax.optimization_barrier((portion, w_rows))
    projected = jnp.concatenate([contract_last(portion, w_gate), contract_last(portion, w_up)], 1)
    pre_gate = projected[:, :hidden_block]
    pre_up = projected[:, hidden_block:]
    gate_sig = jax.nn.sigmoid(pre_gate)
    activated = (pre_gate * gate_sig * pre_up).astype(jnp.bfloat16)
    half_out = lax.psum_scatter(
        jnp.dot(activated, w_down, preferred_element_type=f32).astype(jnp.bfloat16),
        "ctx",
        scatter_dimension=0,
        tiled=True,
    )
    grad_out = out_grad.astype(f32)
    grad_send = jnp.dot(dest_weights.T, grad_out, precision=high).astype(jnp.bfloat16)
    grad_in = lax.all_to_all(grad_send, "ep", split_axis=0, concat_axis=1, tiled=True)
    grad_act = contract_last(lax.all_gather(grad_in, "ctx", axis=0, tiled=True), w_down)
    grad_gate_pre = (grad_act * pre_up * gate_sig * (1.0 + pre_gate * (1.0 - gate_sig))).astype(
        jnp.bfloat16
    )
    grad_up_pre = (grad_act * pre_gate * gate_sig).astype(jnp.bfloat16)
    grad_half = lax.psum_scatter(
        (
            jnp.dot(grad_gate_pre, w_gate, preferred_element_type=f32)
            + jnp.dot(grad_up_pre, w_up, preferred_element_type=f32)
        ).astype(jnp.bfloat16),
        "ctx",
        scatter_dimension=0,
        tiled=True,
    )
    grad_back = lax.all_to_all(grad_half, "ep", split_axis=1, concat_axis=0, tiled=True)
    grad_model_in = jnp.dot(dest_picks, grad_back.astype(f32), precision=high)
    scaled_grad = grad_model_in * gain_cols
    row_parts = jnp.stack(
        [jnp.sum(stream_f * stream_f, -1), jnp.sum(stream_f * scaled_grad, -1)], -1
    )
    row_sums = jnp.sum(gather_blocks(row_parts, "ep"), 0)
    row_scale = lax.rsqrt(row_sums[:, :1] / model_width + 1e-05)
    inner_sum = row_sums[:, 1:]
    grad_stream = (
        grad_out
        + row_scale * scaled_grad
        - stream_f * row_scale**3 * inner_sum / model_width
    ).astype(jnp.bfloat16)
    grad_heads = jnp.einsum(
        "itf,ihf->th", gather_blocks(grad_stream, "ep"), w_rows, preferred_element_type=f32
    )
    head_pull = jax.vjp(lambda value: head_normalize(value, gain_heads), attended)[1]
    grad_attended = head_pull(grad_heads.reshape(tokens_here, head_count, head_size))[0].astype(
        jnp.bfloat16
    )
    state_part = jnp.einsum("thd,the->hde", query3, grad_attended, preferred_element_type=f32)
    half_out, state_part = lax.optimization_barrier((half_out, state_part))
    returned = lax.all_to_all(half_out, "ep", split_axis=1, concat_axis=0, tiled=True)
    expert_mix = jnp.dot(dest_weights, returned.astype(f32), precision=high)
    layer_out = (stream_f + expert_mix).astype(jnp.bfloat16)
    later_sum, state_total = butterfly_sums(state_part, "ctx", True)
    grad_scores = jnp.einsum("the,she->hts", grad_attended, value3, preferred_element_type=f32)
    grad_masked = jnp.where(causal[None], grad_scores, 0.0).astype(jnp.bfloat16)
    grad_att_f = grad_attended.astype(f32)
    grad_query = jnp.einsum("the,hde->thd", grad_att_f, prefix, precision=high) + jnp.einsum(
        "hts,shd->thd", grad_masked, key3, preferred_element_type=f32
    )
    grad_key = jnp.einsum(
        "the,hde->thd", value3.astype(f32), later_sum, precision=high
    ) + jnp.einsum("hts,thd->shd", grad_masked, query3, preferred_element_type=f32)
    grad_value = jnp.einsum(
        "thd,hde->the", key3.astype(f32), later_sum, precision=high
    ) + jnp.einsum("hts,the->she", scores_bf, grad_attended, preferred_element_type=f32)
    flat_shape = (tokens_here, head_count * head_size)
    return (
        layer_out,
        grad_query.astype(jnp.bfloat16).reshape(flat_shape),
        grad_key.astype(jnp.bfloat16).reshape(flat_shape),
        grad_value.astype(jnp.bfloat16).reshape(flat_shape),
        state_total,
        grad_stream,
    )


def solution(mesh):
    return jax.shard_map(
        local,
        mesh=mesh,
        in_specs=(
            P("ctx", "ep"),
            P("ctx", "ep"),
            P("ctx", "ep"),
            P("ep", None, None),
            P("ep"),
            P("ctx", "ep"),
            P("ctx", "ep"),
            P(),
            P("ctx", None),
            P("ctx", None),
            P("ctx", None),
            P("ep", "ctx", None),
            P("ep", "ctx", None),
            P("ep", "ctx", None),
            P("ctx", "ep"),
        ),
        out_specs=(
            P("ctx", "ep"),
            P("ctx", "ep"),
            P("ctx", "ep"),
            P("ctx", "ep"),
            P("ep", None, None),
            P("ctx", "ep"),
        ),
        check_vma=False,
    )
```

```python
import jax
import jax.numpy as jnp
from jax import lax
from jax.sharding import PartitionSpec as P


def butterfly_sums(value, axis, backward):
    count = lax.axis_size(axis)
    place = lax.axis_index(axis)
    total = value
    carried = jnp.zeros_like(value)
    step = 1
    while step < count:
        other = lax.ppermute(total, axis, [(i, i ^ step) for i in range(count)])
        upper = (place & step) != 0
        take = jnp.logical_not(upper) if backward else upper
        carried = carried + jnp.where(take, other, jnp.zeros_like(other))
        total = total + other
        step *= 2
    return carried, total


def gather_doubling(value, axis):
    count = lax.axis_size(axis)
    place = lax.axis_index(axis)
    held = value
    step = 1
    while step < count:
        other = lax.ppermute(held, axis, [(i, i ^ step) for i in range(count)])
        upper = (place & step) != 0
        low = jnp.where(upper, other, held)
        high = jnp.where(upper, held, other)
        held = jnp.concatenate([low, high], 0)
        step *= 2
    return held


def gather_blocks(value, axis):
    count = lax.axis_size(axis)
    spread = jnp.broadcast_to(value[None], (count,) + value.shape)
    return lax.all_to_all(spread, axis, 0, 0, tiled=True)


def head_normalize(attended, gain):
    factor = lax.rsqrt(jnp.mean(attended * attended, -1, keepdims=True) + 1e-06)
    return attended * factor * gain


def contract_last(left, right):
    return lax.dot_general(
        left, right, (((1,), (1,)), ((), ())), preferred_element_type=jnp.float32
    )


def local(
    query_act,
    key_act,
    value_act,
    state_init,
    head_gain,
    out_weight,
    stream_in,
    model_gain,
    expert_ids,
    expert_slots,
    route_gates,
    gate_weight,
    up_weight,
    down_weight,
    out_grad,
):
    f32 = jnp.float32
    high = lax.Precision.HIGHEST
    ep_count = lax.axis_size("ep")
    expert_count = ep_count // 2
    my_ep = lax.axis_index("ep")
    tokens_here = query_act.shape[0]
    head_count = state_init.shape[0]
    head_size = state_init.shape[1]
    model_width = model_gain.shape[0]
    columns = stream_in.shape[1]
    capacity = 5 * tokens_here // (2 * expert_count)
    w_cols = lax.all_gather(out_weight, "ctx", axis=0, tiled=True)
    query3 = query_act.reshape(tokens_here, head_count, head_size)
    key3 = key_act.reshape(tokens_here, head_count, head_size)
    value3 = value_act.reshape(tokens_here, head_count, head_size)
    kv_own = jnp.einsum("thd,the->hde", key3, value3, preferred_element_type=f32)
    before, _ = butterfly_sums(kv_own, "ctx", False)
    prefix = state_init + before
    causal = jnp.arange(tokens_here)[:, None] >= jnp.arange(tokens_here)[None, :]
    scores = jnp.einsum("thd,shd->hts", query3, key3, preferred_element_type=f32)
    scores_bf = jnp.where(causal[None], scores, 0.0).astype(jnp.bfloat16)
    inside = jnp.einsum("hts,she->the", scores_bf, value3, preferred_element_type=f32)
    from_state = jnp.einsum("thd,hde->the", query3.astype(f32), prefix, precision=high)
    attended = from_state + inside
    gain_heads = head_gain.reshape(head_count, head_size)
    normed_heads = (
        head_normalize(attended, gain_heads)
        .astype(jnp.bfloat16)
        .reshape(tokens_here, head_count * head_size)
    )
    w_blocks = w_cols.reshape(ep_count, head_count * head_size, columns)
    attn_proj = jnp.einsum(
        "ith,ihf->tf", gather_blocks(normed_heads, "ep"), w_blocks, preferred_element_type=f32
    )
    stream = (stream_in.astype(f32) + attn_proj).astype(jnp.bfloat16)
    stream_f = stream.astype(f32)
    gain_cols = lax.dynamic_slice_in_dim(model_gain, my_ep * columns, columns, 0)
    dest_expert = jnp.arange(ep_count) % expert_count
    slot_iota = jnp.arange(capacity)
    hits = (expert_ids[:, :, None, None] == dest_expert[None, None, :, None]) & (
        expert_slots[:, :, None, None] == slot_iota[None, None, None, :]
    )
    hits_f = hits.astype(f32)
    dest_picks = jnp.sum(hits_f, 1).reshape(tokens_here, ep_count * capacity)
    dest_weights = jnp.sum(hits_f * route_gates[:, :, None, None], 1).reshape(
        tokens_here, ep_count * capacity
    )
    picked = jnp.dot(
        dest_picks.T.astype(jnp.bfloat16), stream, preferred_element_type=f32
    ).astype(jnp.bfloat16)
    arrived = lax.all_to_all(
        picked.reshape(ep_count, capacity, columns), "ep", 0, 0, tiled=True
    )
    slot_rows = arrived.transpose(1, 0, 2).reshape(capacity, model_width).astype(f32)
    slot_scale = lax.rsqrt(jnp.mean(slot_rows * slot_rows, -1, keepdims=True) + 1e-05)
    expert_in = (slot_rows * slot_scale * model_gain).astype(jnp.bfloat16)
    w_gate = gate_weight[0]
    w_up = up_weight[0]
    w_down = down_weight[0]
    hidden_block = w_gate.shape[0]
    w_rows = lax.all_to_all(w_blocks, "ep", 0, 0, tiled=True)
    portion = lax.all_gather(expert_in, "ctx", axis=0, tiled=True)
    portion, w_rows = lax.optimization_barrier((portion, w_rows))
    projected = jnp.concatenate([contract_last(portion, w_gate), contract_last(portion, w_up)], 1)
    pre_gate = projected[:, :hidden_block]
    pre_up = projected[:, hidden_block:]
    gate_sig = jax.nn.sigmoid(pre_gate)
    activated = (pre_gate * gate_sig * pre_up).astype(jnp.bfloat16)
    half_out = lax.psum_scatter(
        jnp.dot(activated, w_down, preferred_element_type=f32).astype(jnp.bfloat16),
        "ctx",
        scatter_dimension=0,
        tiled=True,
    )
    grad_out = out_grad.astype(f32)
    grad_send = jnp.dot(dest_weights.T, grad_out, precision=high).astype(jnp.bfloat16)
    grad_in = lax.all_to_all(grad_send, "ep", split_axis=0, concat_axis=1, tiled=True)
    grad_act = contract_last(gather_doubling(grad_in, "ctx"), w_down)
    grad_gate_pre = (grad_act * pre_up * gate_sig * (1.0 + pre_gate * (1.0 - gate_sig))).astype(
        jnp.bfloat16
    )
    grad_up_pre = (grad_act * pre_gate * gate_sig).astype(jnp.bfloat16)
    grad_half = lax.psum_scatter(
        (
            jnp.dot(grad_gate_pre, w_gate, preferred_element_type=f32)
            + jnp.dot(grad_up_pre, w_up, preferred_element_type=f32)
        ).astype(jnp.bfloat16),
        "ctx",
        scatter_dimension=0,
        tiled=True,
    )
    grad_back = lax.all_to_all(grad_half, "ep", split_axis=1, concat_axis=0, tiled=True)
    grad_model_in = jnp.dot(dest_picks, grad_back.astype(f32), precision=high)
    scaled_grad = grad_model_in * gain_cols
    row_parts = jnp.stack(
        [jnp.sum(stream_f * stream_f, -1), jnp.sum(stream_f * scaled_grad, -1)], -1
    )
    row_sums = jnp.sum(gather_blocks(row_parts, "ep"), 0)
    row_scale = lax.rsqrt(row_sums[:, :1] / model_width + 1e-05)
    inner_sum = row_sums[:, 1:]
    grad_stream = (
        grad_out
        + row_scale * scaled_grad
        - stream_f * row_scale**3 * inner_sum / model_width
    ).astype(jnp.bfloat16)
    grad_heads = jnp.einsum(
        "itf,ihf->th", gather_blocks(grad_stream, "ep"), w_rows, preferred_element_type=f32
    )
    head_pull = jax.vjp(lambda value: head_normalize(value, gain_heads), attended)[1]
    grad_attended = head_pull(grad_heads.reshape(tokens_here, head_count, head_size))[0].astype(
        jnp.bfloat16
    )
    state_part = jnp.einsum("thd,the->hde", query3, grad_attended, preferred_element_type=f32)
    half_out, state_part = lax.optimization_barrier((half_out, state_part))
    returned = lax.all_to_all(half_out, "ep", split_axis=1, concat_axis=0, tiled=True)
    expert_mix = jnp.dot(dest_weights, returned.astype(f32), precision=high)
    layer_out = (stream_f + expert_mix).astype(jnp.bfloat16)
    later_sum, state_total = butterfly_sums(state_part, "ctx", True)
    grad_scores = jnp.einsum("the,she->hts", grad_attended, value3, preferred_element_type=f32)
    grad_masked = jnp.where(causal[None], grad_scores, 0.0).astype(jnp.bfloat16)
    grad_att_f = grad_attended.astype(f32)
    grad_query = jnp.einsum("the,hde->thd", grad_att_f, prefix, precision=high) + jnp.einsum(
        "hts,shd->thd", grad_masked, key3, preferred_element_type=f32
    )
    grad_key = jnp.einsum(
        "the,hde->thd", value3.astype(f32), later_sum, precision=high
    ) + jnp.einsum("hts,thd->shd", grad_masked, query3, preferred_element_type=f32)
    grad_value = jnp.einsum(
        "thd,hde->the", key3.astype(f32), later_sum, precision=high
    ) + jnp.einsum("hts,the->she", scores_bf, grad_attended, preferred_element_type=f32)
    flat_shape = (tokens_here, head_count * head_size)
    return (
        layer_out,
        grad_query.astype(jnp.bfloat16).reshape(flat_shape),
        grad_key.astype(jnp.bfloat16).reshape(flat_shape),
        grad_value.astype(jnp.bfloat16).reshape(flat_shape),
        state_total,
        grad_stream,
    )


def solution(mesh):
    return jax.shard_map(
        local,
        mesh=mesh,
        in_specs=(
            P("ctx", "ep"),
            P("ctx", "ep"),
            P("ctx", "ep"),
            P("ep", None, None),
            P("ep"),
            P("ctx", "ep"),
            P("ctx", "ep"),
            P(),
            P("ctx", None),
            P("ctx", None),
            P("ctx", None),
            P("ep", "ctx", None),
            P("ep", "ctx", None),
            P("ep", "ctx", None),
            P("ctx", "ep"),
        ),
        out_specs=(
            P("ctx", "ep"),
            P("ctx", "ep"),
            P("ctx", "ep"),
            P("ctx", "ep"),
            P("ep", None, None),
            P("ctx", "ep"),
        ),
        check_vma=False,
    )
```

```python
import jax
import jax.numpy as jnp
from jax import lax
from jax.sharding import PartitionSpec as P


def butterfly_sums(value, axis, backward):
    count = lax.axis_size(axis)
    place = lax.axis_index(axis)
    total = value
    carried = jnp.zeros_like(value)
    step = 1
    while step < count:
        other = lax.ppermute(total, axis, [(i, i ^ step) for i in range(count)])
        upper = (place & step) != 0
        take = jnp.logical_not(upper) if backward else upper
        carried = carried + jnp.where(take, other, jnp.zeros_like(other))
        total = total + other
        step *= 2
    return carried, total


def gather_blocks(value, axis):
    count = lax.axis_size(axis)
    spread = jnp.broadcast_to(value[None], (count,) + value.shape)
    return lax.all_to_all(spread, axis, 0, 0, tiled=True)


def head_normalize(attended, gain):
    factor = lax.rsqrt(jnp.mean(attended * attended, -1, keepdims=True) + 1e-06)
    return attended * factor * gain


def contract_last(left, right):
    return lax.dot_general(
        left, right, (((1,), (1,)), ((), ())), preferred_element_type=jnp.float32
    )


def local(
    query_act,
    key_act,
    value_act,
    state_init,
    head_gain,
    out_weight,
    stream_in,
    model_gain,
    expert_ids,
    expert_slots,
    route_gates,
    gate_weight,
    up_weight,
    down_weight,
    out_grad,
):
    f32 = jnp.float32
    high = lax.Precision.HIGHEST
    ep_count = lax.axis_size("ep")
    expert_count = ep_count // 2
    my_ep = lax.axis_index("ep")
    tokens_here = query_act.shape[0]
    head_count = state_init.shape[0]
    head_size = state_init.shape[1]
    model_width = model_gain.shape[0]
    columns = stream_in.shape[1]
    capacity = 5 * tokens_here // (2 * expert_count)
    dest_expert = jnp.arange(ep_count) % expert_count
    slot_iota = jnp.arange(capacity)
    hits = (expert_ids[:, :, None, None] == dest_expert[None, None, :, None]) & (
        expert_slots[:, :, None, None] == slot_iota[None, None, None, :]
    )
    hits_f = hits.astype(f32)
    dest_picks = jnp.sum(hits_f, 1).reshape(tokens_here, ep_count * capacity)
    dest_weights = jnp.sum(hits_f * route_gates[:, :, None, None], 1).reshape(
        tokens_here, ep_count * capacity
    )
    grad_out = out_grad.astype(f32)
    grad_send = jnp.dot(dest_weights.T, grad_out, precision=high).astype(jnp.bfloat16)
    ctx_count = lax.axis_size("ctx")
    grad_all = lax.all_gather(grad_send, "ctx", axis=0)
    out_weight, grad_all = lax.optimization_barrier((out_weight, grad_all))
    w_cols = lax.all_gather(out_weight, "ctx", axis=0, tiled=True)
    query3 = query_act.reshape(tokens_here, head_count, head_size)
    key3 = key_act.reshape(tokens_here, head_count, head_size)
    value3 = value_act.reshape(tokens_here, head_count, head_size)
    kv_own = jnp.einsum("thd,the->hde", key3, value3, preferred_element_type=f32)
    before, _ = butterfly_sums(kv_own, "ctx", False)
    prefix = state_init + before
    causal = jnp.arange(tokens_here)[:, None] >= jnp.arange(tokens_here)[None, :]
    scores = jnp.einsum("thd,shd->hts", query3, key3, preferred_element_type=f32)
    scores_bf = jnp.where(causal[None], scores, 0.0).astype(jnp.bfloat16)
    inside = jnp.einsum("hts,she->the", scores_bf, value3, preferred_element_type=f32)
    from_state = jnp.einsum("thd,hde->the", query3.astype(f32), prefix, precision=high)
    attended = from_state + inside
    gain_heads = head_gain.reshape(head_count, head_size)
    normed_heads = (
        head_normalize(attended, gain_heads)
        .astype(jnp.bfloat16)
        .reshape(tokens_here, head_count * head_size)
    )
    w_blocks = w_cols.reshape(ep_count, head_count * head_size, columns)
    attn_proj = jnp.einsum(
        "ith,ihf->tf", gather_blocks(normed_heads, "ep"), w_blocks, preferred_element_type=f32
    )
    stream = (stream_in.astype(f32) + attn_proj).astype(jnp.bfloat16)
    stream_f = stream.astype(f32)
    gain_cols = lax.dynamic_slice_in_dim(model_gain, my_ep * columns, columns, 0)
    picked = jnp.dot(
        dest_picks.T.astype(jnp.bfloat16), stream, preferred_element_type=f32
    ).astype(jnp.bfloat16)
    arrived = lax.all_to_all(
        picked.reshape(ep_count, capacity, columns), "ep", 0, 0, tiled=True
    )
    slot_rows = arrived.transpose(1, 0, 2).reshape(capacity, model_width).astype(f32)
    slot_scale = lax.rsqrt(jnp.mean(slot_rows * slot_rows, -1, keepdims=True) + 1e-05)
    expert_in = (slot_rows * slot_scale * model_gain).astype(jnp.bfloat16)
    w_gate = gate_weight[0]
    w_up = up_weight[0]
    w_down = down_weight[0]
    hidden_block = w_gate.shape[0]
    w_rows = lax.all_to_all(w_blocks, "ep", 0, 0, tiled=True)
    portion = lax.all_gather(expert_in, "ctx", axis=0, tiled=True)
    portion, w_rows = lax.optimization_barrier((portion, w_rows))
    projected = jnp.concatenate([contract_last(portion, w_gate), contract_last(portion, w_up)], 1)
    pre_gate = projected[:, :hidden_block]
    pre_up = projected[:, hidden_block:]
    gate_sig = jax.nn.sigmoid(pre_gate)
    activated = (pre_gate * gate_sig * pre_up).astype(jnp.bfloat16)
    half_out = lax.psum_scatter(
        jnp.dot(activated, w_down, preferred_element_type=f32).astype(jnp.bfloat16),
        "ctx",
        scatter_dimension=0,
        tiled=True,
    )
    grad_all = grad_all.reshape(ctx_count, ep_count, capacity, columns).transpose(1, 0, 2, 3)
    grad_in = lax.all_to_all(grad_all, "ep", 0, 0, tiled=True)
    grad_in = grad_in.transpose(1, 2, 0, 3).reshape(ctx_count * capacity, model_width)
    grad_act = contract_last(grad_in, w_down)
    grad_gate_pre = (grad_act * pre_up * gate_sig * (1.0 + pre_gate * (1.0 - gate_sig))).astype(
        jnp.bfloat16
    )
    grad_up_pre = (grad_act * pre_gate * gate_sig).astype(jnp.bfloat16)
    grad_half = lax.psum_scatter(
        (
            jnp.dot(grad_gate_pre, w_gate, preferred_element_type=f32)
            + jnp.dot(grad_up_pre, w_up, preferred_element_type=f32)
        ).astype(jnp.bfloat16),
        "ctx",
        scatter_dimension=0,
        tiled=True,
    )
    grad_back = lax.all_to_all(grad_half, "ep", split_axis=1, concat_axis=0, tiled=True)
    grad_model_in = jnp.dot(dest_picks, grad_back.astype(f32), precision=high)
    scaled_grad = grad_model_in * gain_cols
    row_parts = jnp.stack(
        [jnp.sum(stream_f * stream_f, -1), jnp.sum(stream_f * scaled_grad, -1)], -1
    )
    row_sums = jnp.sum(gather_blocks(row_parts, "ep"), 0)
    row_scale = lax.rsqrt(row_sums[:, :1] / model_width + 1e-05)
    inner_sum = row_sums[:, 1:]
    grad_stream = (
        grad_out
        + row_scale * scaled_grad
        - stream_f * row_scale**3 * inner_sum / model_width
    ).astype(jnp.bfloat16)
    grad_heads = jnp.einsum(
        "itf,ihf->th", gather_blocks(grad_stream, "ep"), w_rows, preferred_element_type=f32
    )
    head_pull = jax.vjp(lambda value: head_normalize(value, gain_heads), attended)[1]
    grad_attended = head_pull(grad_heads.reshape(tokens_here, head_count, head_size))[0].astype(
        jnp.bfloat16
    )
    state_part = jnp.einsum("thd,the->hde", query3, grad_attended, preferred_element_type=f32)
    half_out, state_part = lax.optimization_barrier((half_out, state_part))
    returned = lax.all_to_all(half_out, "ep", split_axis=1, concat_axis=0, tiled=True)
    expert_mix = jnp.dot(dest_weights, returned.astype(f32), precision=high)
    layer_out = (stream_f + expert_mix).astype(jnp.bfloat16)
    later_sum, state_total = butterfly_sums(state_part, "ctx", True)
    grad_scores = jnp.einsum("the,she->hts", grad_attended, value3, preferred_element_type=f32)
    grad_masked = jnp.where(causal[None], grad_scores, 0.0).astype(jnp.bfloat16)
    grad_att_f = grad_attended.astype(f32)
    grad_query = jnp.einsum("the,hde->thd", grad_att_f, prefix, precision=high) + jnp.einsum(
        "hts,shd->thd", grad_masked, key3, preferred_element_type=f32
    )
    grad_key = jnp.einsum(
        "the,hde->thd", value3.astype(f32), later_sum, precision=high
    ) + jnp.einsum("hts,thd->shd", grad_masked, query3, preferred_element_type=f32)
    grad_value = jnp.einsum(
        "thd,hde->the", key3.astype(f32), later_sum, precision=high
    ) + jnp.einsum("hts,the->she", scores_bf, grad_attended, preferred_element_type=f32)
    flat_shape = (tokens_here, head_count * head_size)
    return (
        layer_out,
        grad_query.astype(jnp.bfloat16).reshape(flat_shape),
        grad_key.astype(jnp.bfloat16).reshape(flat_shape),
        grad_value.astype(jnp.bfloat16).reshape(flat_shape),
        state_total,
        grad_stream,
    )


def solution(mesh):
    return jax.shard_map(
        local,
        mesh=mesh,
        in_specs=(
            P("ctx", "ep"),
            P("ctx", "ep"),
            P("ctx", "ep"),
            P("ep", None, None),
            P("ep"),
            P("ctx", "ep"),
            P("ctx", "ep"),
            P(),
            P("ctx", None),
            P("ctx", None),
            P("ctx", None),
            P("ep", "ctx", None),
            P("ep", "ctx", None),
            P("ep", "ctx", None),
            P("ctx", "ep"),
        ),
        out_specs=(
            P("ctx", "ep"),
            P("ctx", "ep"),
            P("ctx", "ep"),
            P("ctx", "ep"),
            P("ep", None, None),
            P("ctx", "ep"),
        ),
        check_vma=False,
    )
```

```python
import jax
import jax.numpy as jnp
from jax import lax
from jax.sharding import PartitionSpec as P


def butterfly_sums(value, axis, backward):
    count = lax.axis_size(axis)
    place = lax.axis_index(axis)
    total = value
    carried = jnp.zeros_like(value)
    step = 1
    while step < count:
        other = lax.ppermute(total, axis, [(i, i ^ step) for i in range(count)])
        upper = (place & step) != 0
        take = jnp.logical_not(upper) if backward else upper
        carried = carried + jnp.where(take, other, jnp.zeros_like(other))
        total = total + other
        step *= 2
    return carried, total


def gather_blocks(value, axis):
    count = lax.axis_size(axis)
    spread = jnp.broadcast_to(value[None], (count,) + value.shape)
    return lax.all_to_all(spread, axis, 0, 0, tiled=True)


def scatter_sum(value, axis):
    count = lax.axis_size(axis)
    rows, width = value.shape
    block = rows // count
    dense = value.reshape(count, block * width // 128, 128)
    part = lax.psum_scatter(dense, axis, scatter_dimension=0, tiled=True)
    return part.reshape(block, width)


def head_normalize(attended, gain):
    factor = lax.rsqrt(jnp.mean(attended * attended, -1, keepdims=True) + 1e-06)
    return attended * factor * gain


def contract_last(left, right):
    return lax.dot_general(
        left, right, (((1,), (1,)), ((), ())), preferred_element_type=jnp.float32
    )


def local(
    query_act,
    key_act,
    value_act,
    state_init,
    head_gain,
    out_weight,
    stream_in,
    model_gain,
    expert_ids,
    expert_slots,
    route_gates,
    gate_weight,
    up_weight,
    down_weight,
    out_grad,
):
    f32 = jnp.float32
    high = lax.Precision.HIGHEST
    ep_count = lax.axis_size("ep")
    expert_count = ep_count // 2
    my_ep = lax.axis_index("ep")
    tokens_here = query_act.shape[0]
    head_count = state_init.shape[0]
    head_size = state_init.shape[1]
    model_width = model_gain.shape[0]
    columns = stream_in.shape[1]
    capacity = 5 * tokens_here // (2 * expert_count)
    w_cols = lax.all_gather(out_weight, "ctx", axis=0, tiled=True)
    query3 = query_act.reshape(tokens_here, head_count, head_size)
    key3 = key_act.reshape(tokens_here, head_count, head_size)
    value3 = value_act.reshape(tokens_here, head_count, head_size)
    kv_own = jnp.einsum("thd,the->hde", key3, value3, preferred_element_type=f32)
    before, _ = butterfly_sums(kv_own, "ctx", False)
    prefix = state_init + before
    causal = jnp.arange(tokens_here)[:, None] >= jnp.arange(tokens_here)[None, :]
    scores = jnp.einsum("thd,shd->hts", query3, key3, preferred_element_type=f32)
    scores_bf = jnp.where(causal[None], scores, 0.0).astype(jnp.bfloat16)
    inside = jnp.einsum("hts,she->the", scores_bf, value3, preferred_element_type=f32)
    from_state = jnp.einsum("thd,hde->the", query3.astype(f32), prefix, precision=high)
    attended = from_state + inside
    gain_heads = head_gain.reshape(head_count, head_size)
    normed_heads = (
        head_normalize(attended, gain_heads)
        .astype(jnp.bfloat16)
        .reshape(tokens_here, head_count * head_size)
    )
    w_blocks = w_cols.reshape(ep_count, head_count * head_size, columns)
    attn_proj = jnp.einsum(
        "ith,ihf->tf", gather_blocks(normed_heads, "ep"), w_blocks, preferred_element_type=f32
    )
    stream = (stream_in.astype(f32) + attn_proj).astype(jnp.bfloat16)
    stream_f = stream.astype(f32)
    gain_cols = lax.dynamic_slice_in_dim(model_gain, my_ep * columns, columns, 0)
    dest_expert = jnp.arange(ep_count) % expert_count
    slot_iota = jnp.arange(capacity)
    hits = (expert_ids[:, :, None, None] == dest_expert[None, None, :, None]) & (
        expert_slots[:, :, None, None] == slot_iota[None, None, None, :]
    )
    hits_f = hits.astype(f32)
    dest_picks = jnp.sum(hits_f, 1).reshape(tokens_here, ep_count * capacity)
    dest_weights = jnp.sum(hits_f * route_gates[:, :, None, None], 1).reshape(
        tokens_here, ep_count * capacity
    )
    picked = jnp.dot(
        dest_picks.T.astype(jnp.bfloat16), stream, preferred_element_type=f32
    ).astype(jnp.bfloat16)
    arrived = lax.all_to_all(
        picked.reshape(ep_count, capacity, columns), "ep", 0, 0, tiled=True
    )
    slot_rows = arrived.transpose(1, 0, 2).reshape(capacity, model_width).astype(f32)
    slot_scale = lax.rsqrt(jnp.mean(slot_rows * slot_rows, -1, keepdims=True) + 1e-05)
    expert_in = (slot_rows * slot_scale * model_gain).astype(jnp.bfloat16)
    w_gate = gate_weight[0]
    w_up = up_weight[0]
    w_down = down_weight[0]
    hidden_block = w_gate.shape[0]
    w_rows = lax.all_to_all(w_blocks, "ep", 0, 0, tiled=True)
    portion = lax.all_gather(expert_in, "ctx", axis=0, tiled=True)
    square_sums = jnp.sum(gather_blocks(jnp.sum(stream_f * stream_f, -1, keepdims=True), "ep"), 0)
    portion, w_rows, square_sums = lax.optimization_barrier((portion, w_rows, square_sums))
    row_scale = lax.rsqrt(square_sums / model_width + 1e-05)
    projected = jnp.concatenate([contract_last(portion, w_gate), contract_last(portion, w_up)], 1)
    pre_gate = projected[:, :hidden_block]
    pre_up = projected[:, hidden_block:]
    gate_sig = jax.nn.sigmoid(pre_gate)
    activated = (pre_gate * gate_sig * pre_up).astype(jnp.bfloat16)
    half_out = scatter_sum(
        jnp.dot(activated, w_down, preferred_element_type=f32).astype(jnp.bfloat16), "ctx"
    )
    grad_out = out_grad.astype(f32)
    grad_send = jnp.dot(dest_weights.T, grad_out, precision=high).astype(jnp.bfloat16)
    grad_in = lax.all_to_all(grad_send, "ep", split_axis=0, concat_axis=1, tiled=True)
    grad_act = contract_last(lax.all_gather(grad_in, "ctx", axis=0, tiled=True), w_down)
    grad_gate_pre = (grad_act * pre_up * gate_sig * (1.0 + pre_gate * (1.0 - gate_sig))).astype(
        jnp.bfloat16
    )
    grad_up_pre = (grad_act * pre_gate * gate_sig).astype(jnp.bfloat16)
    grad_half = scatter_sum(
        (
            jnp.dot(grad_gate_pre, w_gate, preferred_element_type=f32)
            + jnp.dot(grad_up_pre, w_up, preferred_element_type=f32)
        ).astype(jnp.bfloat16),
        "ctx",
    )
    slot_inner = jnp.sum(slot_rows * model_gain * grad_half.astype(f32), -1, keepdims=True)
    inner_hi = slot_inner.astype(jnp.bfloat16)
    inner_lo = (slot_inner - inner_hi.astype(f32)).astype(jnp.bfloat16)
    inner_pair = jnp.broadcast_to(
        jnp.concatenate([inner_hi, inner_lo], -1)[:, None, :], (capacity, ep_count, 2)
    )
    payload = jnp.concatenate([grad_half.reshape(capacity, ep_count, columns), inner_pair], -1)
    grad_back = lax.all_to_all(payload, "ep", split_axis=1, concat_axis=0, tiled=True)
    grad_back = grad_back.reshape(ep_count * capacity, columns + 2).astype(f32)
    grad_model_in = jnp.dot(dest_picks, grad_back[:, :columns], precision=high)
    scaled_grad = grad_model_in * gain_cols
    inner_sum = jnp.dot(
        dest_picks, grad_back[:, columns:columns + 1] + grad_back[:, columns + 1:], precision=high
    )
    grad_stream = (
        grad_out
        + row_scale * scaled_grad
        - stream_f * row_scale**3 * inner_sum / model_width
    ).astype(jnp.bfloat16)
    grad_heads = jnp.einsum(
        "itf,ihf->th", gather_blocks(grad_stream, "ep"), w_rows, preferred_element_type=f32
    )
    head_pull = jax.vjp(lambda value: head_normalize(value, gain_heads), attended)[1]
    grad_attended = head_pull(grad_heads.reshape(tokens_here, head_count, head_size))[0].astype(
        jnp.bfloat16
    )
    state_part = jnp.einsum("thd,the->hde", query3, grad_attended, preferred_element_type=f32)
    half_out, state_part = lax.optimization_barrier((half_out, state_part))
    returned = lax.all_to_all(half_out, "ep", split_axis=1, concat_axis=0, tiled=True)
    expert_mix = jnp.dot(dest_weights, returned.astype(f32), precision=high)
    layer_out = (stream_f + expert_mix).astype(jnp.bfloat16)
    later_sum, state_total = butterfly_sums(state_part, "ctx", True)
    grad_scores = jnp.einsum("the,she->hts", grad_attended, value3, preferred_element_type=f32)
    grad_masked = jnp.where(causal[None], grad_scores, 0.0).astype(jnp.bfloat16)
    grad_att_f = grad_attended.astype(f32)
    grad_query = jnp.einsum("the,hde->thd", grad_att_f, prefix, precision=high) + jnp.einsum(
        "hts,shd->thd", grad_masked, key3, preferred_element_type=f32
    )
    grad_key = jnp.einsum(
        "the,hde->thd", value3.astype(f32), later_sum, precision=high
    ) + jnp.einsum("hts,thd->shd", grad_masked, query3, preferred_element_type=f32)
    grad_value = jnp.einsum(
        "thd,hde->the", key3.astype(f32), later_sum, precision=high
    ) + jnp.einsum("hts,the->she", scores_bf, grad_attended, preferred_element_type=f32)
    flat_shape = (tokens_here, head_count * head_size)
    return (
        layer_out,
        grad_query.astype(jnp.bfloat16).reshape(flat_shape),
        grad_key.astype(jnp.bfloat16).reshape(flat_shape),
        grad_value.astype(jnp.bfloat16).reshape(flat_shape),
        state_total,
        grad_stream,
    )


def solution(mesh):
    return jax.shard_map(
        local,
        mesh=mesh,
        in_specs=(
            P("ctx", "ep"),
            P("ctx", "ep"),
            P("ctx", "ep"),
            P("ep", None, None),
            P("ep"),
            P("ctx", "ep"),
            P("ctx", "ep"),
            P(),
            P("ctx", None),
            P("ctx", None),
            P("ctx", None),
            P("ep", "ctx", None),
            P("ep", "ctx", None),
            P("ep", "ctx", None),
            P("ctx", "ep"),
        ),
        out_specs=(
            P("ctx", "ep"),
            P("ctx", "ep"),
            P("ctx", "ep"),
            P("ctx", "ep"),
            P("ep", None, None),
            P("ctx", "ep"),
        ),
        check_vma=False,
    )
```

```python
import jax
import jax.numpy as jnp
from jax import lax
from jax.sharding import PartitionSpec as P


def butterfly_sums(value, axis, backward, ride=None):
    count = lax.axis_size(axis)
    place = lax.axis_index(axis)
    total = value
    carried = jnp.zeros_like(value)
    step = 1
    while step < count:
        other = lax.ppermute(total, axis, [(i, i ^ step) for i in range(count)])
        if ride is not None and step == 1:
            other, ride = lax.optimization_barrier((other, ride))
        upper = (place & step) != 0
        take = jnp.logical_not(upper) if backward else upper
        carried = carried + jnp.where(take, other, jnp.zeros_like(other))
        total = total + other
        step *= 2
    if ride is not None:
        return carried, total, ride
    return carried, total


def gather_blocks(value, axis):
    count = lax.axis_size(axis)
    spread = jnp.broadcast_to(value[None], (count,) + value.shape)
    return lax.all_to_all(spread, axis, 0, 0, tiled=True)


def scatter_sum(value, axis):
    count = lax.axis_size(axis)
    rows, width = value.shape
    block = rows // count
    dense = value.reshape(count, block * width // 128, 128)
    part = lax.psum_scatter(dense, axis, scatter_dimension=0, tiled=True)
    return part.reshape(block, width)


def head_normalize(attended, gain):
    factor = lax.rsqrt(jnp.mean(attended * attended, -1, keepdims=True) + 1e-06)
    return attended * factor * gain


def contract_last(left, right):
    return lax.dot_general(
        left, right, (((1,), (1,)), ((), ())), preferred_element_type=jnp.float32
    )


def local(
    query_act,
    key_act,
    value_act,
    state_init,
    head_gain,
    out_weight,
    stream_in,
    model_gain,
    expert_ids,
    expert_slots,
    route_gates,
    gate_weight,
    up_weight,
    down_weight,
    out_grad,
):
    f32 = jnp.float32
    high = lax.Precision.HIGHEST
    ep_count = lax.axis_size("ep")
    expert_count = ep_count // 2
    my_ep = lax.axis_index("ep")
    tokens_here = query_act.shape[0]
    head_count = state_init.shape[0]
    head_size = state_init.shape[1]
    model_width = model_gain.shape[0]
    columns = stream_in.shape[1]
    capacity = 5 * tokens_here // (2 * expert_count)
    w_cols = lax.all_gather(out_weight, "ctx", axis=0, tiled=True)
    query3 = query_act.reshape(tokens_here, head_count, head_size)
    key3 = key_act.reshape(tokens_here, head_count, head_size)
    value3 = value_act.reshape(tokens_here, head_count, head_size)
    kv_own = jnp.einsum("thd,the->hde", key3, value3, preferred_element_type=f32)
    before, _ = butterfly_sums(kv_own, "ctx", False)
    prefix = state_init + before
    causal = jnp.arange(tokens_here)[:, None] >= jnp.arange(tokens_here)[None, :]
    scores = jnp.einsum("thd,shd->hts", query3, key3, preferred_element_type=f32)
    scores_bf = jnp.where(causal[None], scores, 0.0).astype(jnp.bfloat16)
    inside = jnp.einsum("hts,she->the", scores_bf, value3, preferred_element_type=f32)
    from_state = jnp.einsum("thd,hde->the", query3.astype(f32), prefix, precision=high)
    attended = from_state + inside
    gain_heads = head_gain.reshape(head_count, head_size)
    normed_heads = (
        head_normalize(attended, gain_heads)
        .astype(jnp.bfloat16)
        .reshape(tokens_here, head_count * head_size)
    )
    w_blocks = w_cols.reshape(ep_count, head_count * head_size, columns)
    attn_proj = jnp.einsum(
        "ith,ihf->tf", gather_blocks(normed_heads, "ep"), w_blocks, preferred_element_type=f32
    )
    stream = (stream_in.astype(f32) + attn_proj).astype(jnp.bfloat16)
    stream_f = stream.astype(f32)
    gain_cols = lax.dynamic_slice_in_dim(model_gain, my_ep * columns, columns, 0)
    dest_expert = jnp.arange(ep_count) % expert_count
    slot_iota = jnp.arange(capacity)
    hits = (expert_ids[:, :, None, None] == dest_expert[None, None, :, None]) & (
        expert_slots[:, :, None, None] == slot_iota[None, None, None, :]
    )
    hits_f = hits.astype(f32)
    dest_picks = jnp.sum(hits_f, 1).reshape(tokens_here, ep_count * capacity)
    dest_weights = jnp.sum(hits_f * route_gates[:, :, None, None], 1).reshape(
        tokens_here, ep_count * capacity
    )
    picked = jnp.dot(
        dest_picks.T.astype(jnp.bfloat16), stream, preferred_element_type=f32
    ).astype(jnp.bfloat16)
    arrived = lax.all_to_all(
        picked.reshape(ep_count, capacity, columns), "ep", 0, 0, tiled=True
    )
    slot_rows = arrived.transpose(1, 0, 2).reshape(capacity, model_width).astype(f32)
    slot_scale = lax.rsqrt(jnp.mean(slot_rows * slot_rows, -1, keepdims=True) + 1e-05)
    expert_in = (slot_rows * slot_scale * model_gain).astype(jnp.bfloat16)
    w_gate = gate_weight[0]
    w_up = up_weight[0]
    w_down = down_weight[0]
    hidden_block = w_gate.shape[0]
    w_rows = lax.all_to_all(w_blocks, "ep", 0, 0, tiled=True)
    portion = lax.all_gather(expert_in, "ctx", axis=0, tiled=True)
    square_sums = jnp.sum(gather_blocks(jnp.sum(stream_f * stream_f, -1, keepdims=True), "ep"), 0)
    portion, w_rows, square_sums = lax.optimization_barrier((portion, w_rows, square_sums))
    row_scale = lax.rsqrt(square_sums / model_width + 1e-05)
    projected = jnp.concatenate([contract_last(portion, w_gate), contract_last(portion, w_up)], 1)
    pre_gate = projected[:, :hidden_block]
    pre_up = projected[:, hidden_block:]
    gate_sig = jax.nn.sigmoid(pre_gate)
    activated = (pre_gate * gate_sig * pre_up).astype(jnp.bfloat16)
    half_out = scatter_sum(
        jnp.dot(activated, w_down, preferred_element_type=f32).astype(jnp.bfloat16), "ctx"
    )
    grad_out = out_grad.astype(f32)
    grad_send = jnp.dot(dest_weights.T, grad_out, precision=high).astype(jnp.bfloat16)
    grad_in = lax.all_to_all(grad_send, "ep", split_axis=0, concat_axis=1, tiled=True)
    grad_act = contract_last(lax.all_gather(grad_in, "ctx", axis=0, tiled=True), w_down)
    grad_gate_pre = (grad_act * pre_up * gate_sig * (1.0 + pre_gate * (1.0 - gate_sig))).astype(
        jnp.bfloat16
    )
    grad_up_pre = (grad_act * pre_gate * gate_sig).astype(jnp.bfloat16)
    grad_half = scatter_sum(
        (
            jnp.dot(grad_gate_pre, w_gate, preferred_element_type=f32)
            + jnp.dot(grad_up_pre, w_up, preferred_element_type=f32)
        ).astype(jnp.bfloat16),
        "ctx",
    )
    slot_inner = jnp.sum(slot_rows * model_gain * grad_half.astype(f32), -1, keepdims=True)
    inner_hi = slot_inner.astype(jnp.bfloat16)
    inner_lo = (slot_inner - inner_hi.astype(f32)).astype(jnp.bfloat16)
    inner_pair = jnp.broadcast_to(
        jnp.concatenate([inner_hi, inner_lo], -1)[:, None, :], (capacity, ep_count, 2)
    )
    payload = jnp.concatenate([grad_half.reshape(capacity, ep_count, columns), inner_pair], -1)
    grad_back = lax.all_to_all(payload, "ep", split_axis=1, concat_axis=0, tiled=True)
    grad_back = grad_back.reshape(ep_count * capacity, columns + 2).astype(f32)
    grad_model_in = jnp.dot(dest_picks, grad_back[:, :columns], precision=high)
    scaled_grad = grad_model_in * gain_cols
    inner_sum = jnp.dot(
        dest_picks, grad_back[:, columns:columns + 1] + grad_back[:, columns + 1:], precision=high
    )
    grad_stream = (
        grad_out
        + row_scale * scaled_grad
        - stream_f * row_scale**3 * inner_sum / model_width
    ).astype(jnp.bfloat16)
    grad_heads = jnp.einsum(
        "itf,ihf->th", gather_blocks(grad_stream, "ep"), w_rows, preferred_element_type=f32
    )
    head_pull = jax.vjp(lambda value: head_normalize(value, gain_heads), attended)[1]
    grad_attended = head_pull(grad_heads.reshape(tokens_here, head_count, head_size))[0].astype(
        jnp.bfloat16
    )
    state_part = jnp.einsum("thd,the->hde", query3, grad_attended, preferred_element_type=f32)
    later_sum, state_total, half_out = butterfly_sums(state_part, "ctx", True, half_out)
    returned = lax.all_to_all(half_out, "ep", split_axis=1, concat_axis=0, tiled=True)
    expert_mix = jnp.dot(dest_weights, returned.astype(f32), precision=high)
    layer_out = (stream_f + expert_mix).astype(jnp.bfloat16)
    grad_scores = jnp.einsum("the,she->hts", grad_attended, value3, preferred_element_type=f32)
    grad_masked = jnp.where(causal[None], grad_scores, 0.0).astype(jnp.bfloat16)
    grad_att_f = grad_attended.astype(f32)
    grad_query = jnp.einsum("the,hde->thd", grad_att_f, prefix, precision=high) + jnp.einsum(
        "hts,shd->thd", grad_masked, key3, preferred_element_type=f32
    )
    grad_key = jnp.einsum(
        "the,hde->thd", value3.astype(f32), later_sum, precision=high
    ) + jnp.einsum("hts,thd->shd", grad_masked, query3, preferred_element_type=f32)
    grad_value = jnp.einsum(
        "thd,hde->the", key3.astype(f32), later_sum, precision=high
    ) + jnp.einsum("hts,the->she", scores_bf, grad_attended, preferred_element_type=f32)
    flat_shape = (tokens_here, head_count * head_size)
    return (
        layer_out,
        grad_query.astype(jnp.bfloat16).reshape(flat_shape),
        grad_key.astype(jnp.bfloat16).reshape(flat_shape),
        grad_value.astype(jnp.bfloat16).reshape(flat_shape),
        state_total,
        grad_stream,
    )


def solution(mesh):
    return jax.shard_map(
        local,
        mesh=mesh,
        in_specs=(
            P("ctx", "ep"),
            P("ctx", "ep"),
            P("ctx", "ep"),
            P("ep", None, None),
            P("ep"),
            P("ctx", "ep"),
            P("ctx", "ep"),
            P(),
            P("ctx", None),
            P("ctx", None),
            P("ctx", None),
            P("ep", "ctx", None),
            P("ep", "ctx", None),
            P("ep", "ctx", None),
            P("ctx", "ep"),
        ),
        out_specs=(
            P("ctx", "ep"),
            P("ctx", "ep"),
            P("ctx", "ep"),
            P("ctx", "ep"),
            P("ep", None, None),
            P("ctx", "ep"),
        ),
        check_vma=False,
    )
```

```python
import jax
import jax.numpy as jnp
from jax import lax
from jax.sharding import PartitionSpec as P


def butterfly_sums(value, axis, backward):
    count = lax.axis_size(axis)
    place = lax.axis_index(axis)
    total = value
    carried = jnp.zeros_like(value)
    step = 1
    while step < count:
        other = lax.ppermute(total, axis, [(i, i ^ step) for i in range(count)])
        upper = (place & step) != 0
        take = jnp.logical_not(upper) if backward else upper
        carried = carried + jnp.where(take, other, jnp.zeros_like(other))
        total = total + other
        step *= 2
    return carried, total


def gather_blocks(value, axis):
    count = lax.axis_size(axis)
    spread = jnp.broadcast_to(value[None], (count,) + value.shape)
    return lax.all_to_all(spread, axis, 0, 0, tiled=True)


def scatter_sum(value, axis):
    count = lax.axis_size(axis)
    parts, rows, width = value.shape
    block = rows // count
    dense = value.reshape(parts, count, block, width).transpose(1, 0, 2, 3)
    dense = dense.reshape(count, parts * block * width // 128, 128)
    part = lax.psum_scatter(dense, axis, scatter_dimension=0, tiled=True)
    return part.reshape(parts, block, width)


def head_normalize(attended, gain):
    factor = lax.rsqrt(jnp.mean(attended * attended, -1, keepdims=True) + 1e-06)
    return attended * factor * gain


def contract_last(left, right):
    return lax.dot_general(
        left, right, (((1,), (1,)), ((), ())), preferred_element_type=jnp.float32
    )


def local(
    query_act,
    key_act,
    value_act,
    state_init,
    head_gain,
    out_weight,
    stream_in,
    model_gain,
    expert_ids,
    expert_slots,
    route_gates,
    gate_weight,
    up_weight,
    down_weight,
    out_grad,
):
    f32 = jnp.float32
    high = lax.Precision.HIGHEST
    ep_count = lax.axis_size("ep")
    expert_count = ep_count // 2
    my_ep = lax.axis_index("ep")
    tokens_here = query_act.shape[0]
    head_count = state_init.shape[0]
    head_size = state_init.shape[1]
    model_width = model_gain.shape[0]
    columns = stream_in.shape[1]
    capacity = 5 * tokens_here // (2 * expert_count)
    w_cols = lax.all_gather(out_weight, "ctx", axis=0, tiled=True)
    query3 = query_act.reshape(tokens_here, head_count, head_size)
    key3 = key_act.reshape(tokens_here, head_count, head_size)
    value3 = value_act.reshape(tokens_here, head_count, head_size)
    kv_own = jnp.einsum("thd,the->hde", key3, value3, preferred_element_type=f32)
    before, _ = butterfly_sums(kv_own, "ctx", False)
    prefix = state_init + before
    causal = jnp.arange(tokens_here)[:, None] >= jnp.arange(tokens_here)[None, :]
    scores = jnp.einsum("thd,shd->hts", query3, key3, preferred_element_type=f32)
    scores_bf = jnp.where(causal[None], scores, 0.0).astype(jnp.bfloat16)
    inside = jnp.einsum("hts,she->the", scores_bf, value3, preferred_element_type=f32)
    from_state = jnp.einsum("thd,hde->the", query3.astype(f32), prefix, precision=high)
    attended = from_state + inside
    gain_heads = head_gain.reshape(head_count, head_size)
    normed_heads = (
        head_normalize(attended, gain_heads)
        .astype(jnp.bfloat16)
        .reshape(tokens_here, head_count * head_size)
    )
    w_blocks = w_cols.reshape(ep_count, head_count * head_size, columns)
    attn_proj = jnp.einsum(
        "ith,ihf->tf", gather_blocks(normed_heads, "ep"), w_blocks, preferred_element_type=f32
    )
    stream = (stream_in.astype(f32) + attn_proj).astype(jnp.bfloat16)
    stream_f = stream.astype(f32)
    gain_cols = lax.dynamic_slice_in_dim(model_gain, my_ep * columns, columns, 0)
    dest_expert = jnp.arange(ep_count) % expert_count
    slot_iota = jnp.arange(capacity)
    hits = (expert_ids[:, :, None, None] == dest_expert[None, None, :, None]) & (
        expert_slots[:, :, None, None] == slot_iota[None, None, None, :]
    )
    hits_f = hits.astype(f32)
    dest_picks = jnp.sum(hits_f, 1).reshape(tokens_here, ep_count * capacity)
    dest_weights = jnp.sum(hits_f * route_gates[:, :, None, None], 1).reshape(
        tokens_here, ep_count * capacity
    )
    picked = jnp.dot(
        dest_picks.T.astype(jnp.bfloat16), stream, preferred_element_type=f32
    ).astype(jnp.bfloat16)
    arrived = lax.all_to_all(
        picked.reshape(ep_count, capacity, columns), "ep", 0, 0, tiled=True
    )
    slot_rows = arrived.transpose(1, 0, 2).reshape(capacity, model_width).astype(f32)
    slot_scale = lax.rsqrt(jnp.mean(slot_rows * slot_rows, -1, keepdims=True) + 1e-05)
    expert_in = (slot_rows * slot_scale * model_gain).astype(jnp.bfloat16)
    w_gate = gate_weight[0]
    w_up = up_weight[0]
    w_down = down_weight[0]
    hidden_block = w_gate.shape[0]
    w_rows = lax.all_to_all(w_blocks, "ep", 0, 0, tiled=True)
    portion = lax.all_gather(expert_in, "ctx", axis=0, tiled=True)
    square_sums = jnp.sum(gather_blocks(jnp.sum(stream_f * stream_f, -1, keepdims=True), "ep"), 0)
    portion, w_rows, square_sums = lax.optimization_barrier((portion, w_rows, square_sums))
    row_scale = lax.rsqrt(square_sums / model_width + 1e-05)
    projected = jnp.concatenate([contract_last(portion, w_gate), contract_last(portion, w_up)], 1)
    pre_gate = projected[:, :hidden_block]
    pre_up = projected[:, hidden_block:]
    gate_sig = jax.nn.sigmoid(pre_gate)
    activated = (pre_gate * gate_sig * pre_up).astype(jnp.bfloat16)
    out_terms = jnp.dot(activated, w_down, preferred_element_type=f32).astype(jnp.bfloat16)
    grad_out = out_grad.astype(f32)
    grad_send = jnp.dot(dest_weights.T, grad_out, precision=high).astype(jnp.bfloat16)
    grad_in = lax.all_to_all(grad_send, "ep", split_axis=0, concat_axis=1, tiled=True)
    grad_act = contract_last(lax.all_gather(grad_in, "ctx", axis=0, tiled=True), w_down)
    grad_gate_pre = (grad_act * pre_up * gate_sig * (1.0 + pre_gate * (1.0 - gate_sig))).astype(
        jnp.bfloat16
    )
    grad_up_pre = (grad_act * pre_gate * gate_sig).astype(jnp.bfloat16)
    grad_terms = (
        jnp.dot(grad_gate_pre, w_gate, preferred_element_type=f32)
        + jnp.dot(grad_up_pre, w_up, preferred_element_type=f32)
    ).astype(jnp.bfloat16)
    both_halves = scatter_sum(jnp.stack([out_terms, grad_terms]), "ctx")
    half_out = both_halves[0]
    grad_half = both_halves[1]
    slot_inner = jnp.sum(slot_rows * model_gain * grad_half.astype(f32), -1, keepdims=True)
    inner_hi = slot_inner.astype(jnp.bfloat16)
    inner_lo = (slot_inner - inner_hi.astype(f32)).astype(jnp.bfloat16)
    inner_pair = jnp.broadcast_to(
        jnp.concatenate([inner_hi, inner_lo], -1)[:, None, :], (capacity, ep_count, 2)
    )
    payload = jnp.concatenate([grad_half.reshape(capacity, ep_count, columns), inner_pair], -1)
    grad_back = lax.all_to_all(payload, "ep", split_axis=1, concat_axis=0, tiled=True)
    grad_back = grad_back.reshape(ep_count * capacity, columns + 2).astype(f32)
    grad_model_in = jnp.dot(dest_picks, grad_back[:, :columns], precision=high)
    scaled_grad = grad_model_in * gain_cols
    inner_sum = jnp.dot(
        dest_picks, grad_back[:, columns:columns + 1] + grad_back[:, columns + 1:], precision=high
    )
    grad_stream = (
        grad_out
        + row_scale * scaled_grad
        - stream_f * row_scale**3 * inner_sum / model_width
    ).astype(jnp.bfloat16)
    grad_heads = jnp.einsum(
        "itf,ihf->th", gather_blocks(grad_stream, "ep"), w_rows, preferred_element_type=f32
    )
    head_pull = jax.vjp(lambda value: head_normalize(value, gain_heads), attended)[1]
    grad_attended = head_pull(grad_heads.reshape(tokens_here, head_count, head_size))[0].astype(
        jnp.bfloat16
    )
    state_part = jnp.einsum("thd,the->hde", query3, grad_attended, preferred_element_type=f32)
    half_out, state_part = lax.optimization_barrier((half_out, state_part))
    returned = lax.all_to_all(half_out, "ep", split_axis=1, concat_axis=0, tiled=True)
    expert_mix = jnp.dot(dest_weights, returned.astype(f32), precision=high)
    layer_out = (stream_f + expert_mix).astype(jnp.bfloat16)
    later_sum, state_total = butterfly_sums(state_part, "ctx", True)
    grad_scores = jnp.einsum("the,she->hts", grad_attended, value3, preferred_element_type=f32)
    grad_masked = jnp.where(causal[None], grad_scores, 0.0).astype(jnp.bfloat16)
    grad_att_f = grad_attended.astype(f32)
    grad_query = jnp.einsum("the,hde->thd", grad_att_f, prefix, precision=high) + jnp.einsum(
        "hts,shd->thd", grad_masked, key3, preferred_element_type=f32
    )
    grad_key = jnp.einsum(
        "the,hde->thd", value3.astype(f32), later_sum, precision=high
    ) + jnp.einsum("hts,thd->shd", grad_masked, query3, preferred_element_type=f32)
    grad_value = jnp.einsum(
        "thd,hde->the", key3.astype(f32), later_sum, precision=high
    ) + jnp.einsum("hts,the->she", scores_bf, grad_attended, preferred_element_type=f32)
    flat_shape = (tokens_here, head_count * head_size)
    return (
        layer_out,
        grad_query.astype(jnp.bfloat16).reshape(flat_shape),
        grad_key.astype(jnp.bfloat16).reshape(flat_shape),
        grad_value.astype(jnp.bfloat16).reshape(flat_shape),
        state_total,
        grad_stream,
    )


def solution(mesh):
    return jax.shard_map(
        local,
        mesh=mesh,
        in_specs=(
            P("ctx", "ep"),
            P("ctx", "ep"),
            P("ctx", "ep"),
            P("ep", None, None),
            P("ep"),
            P("ctx", "ep"),
            P("ctx", "ep"),
            P(),
            P("ctx", None),
            P("ctx", None),
            P("ctx", None),
            P("ep", "ctx", None),
            P("ep", "ctx", None),
            P("ep", "ctx", None),
            P("ctx", "ep"),
        ),
        out_specs=(
            P("ctx", "ep"),
            P("ctx", "ep"),
            P("ctx", "ep"),
            P("ctx", "ep"),
            P("ep", None, None),
            P("ctx", "ep"),
        ),
        check_vma=False,
    )
```

```python
import jax
import jax.numpy as jnp
from jax import lax
from jax.sharding import PartitionSpec as P


def butterfly_sums(value, axis, backward):
    count = lax.axis_size(axis)
    place = lax.axis_index(axis)
    total = value
    carried = jnp.zeros_like(value)
    step = 1
    while step < count:
        other = lax.ppermute(total, axis, [(i, i ^ step) for i in range(count)])
        upper = (place & step) != 0
        take = jnp.logical_not(upper) if backward else upper
        carried = carried + jnp.where(take, other, jnp.zeros_like(other))
        total = total + other
        step *= 2
    return carried, total


def gather_blocks(value, axis):
    count = lax.axis_size(axis)
    spread = jnp.broadcast_to(value[None], (count,) + value.shape)
    return lax.all_to_all(spread, axis, 0, 0, tiled=True)


def scatter_sum(values, axis):
    count = lax.axis_size(axis)
    rows, width = values[0].shape
    block = rows // count
    joined = jnp.concatenate([value.reshape(count, block, width) for value in values], 1)
    part = lax.psum_scatter(joined, axis, scatter_dimension=0, tiled=True)
    return [part[0, i * block:(i + 1) * block] for i in range(len(values))]


def head_normalize(attended, gain):
    factor = lax.rsqrt(jnp.mean(attended * attended, -1, keepdims=True) + 1e-06)
    return attended * factor * gain


def contract_last(left, right):
    return lax.dot_general(
        left, right, (((1,), (1,)), ((), ())), preferred_element_type=jnp.float32
    )


def local(
    query_act,
    key_act,
    value_act,
    state_init,
    head_gain,
    out_weight,
    stream_in,
    model_gain,
    expert_ids,
    expert_slots,
    route_gates,
    gate_weight,
    up_weight,
    down_weight,
    out_grad,
):
    f32 = jnp.float32
    high = lax.Precision.HIGHEST
    ep_count = lax.axis_size("ep")
    expert_count = ep_count // 2
    my_ep = lax.axis_index("ep")
    tokens_here = query_act.shape[0]
    head_count = state_init.shape[0]
    head_size = state_init.shape[1]
    model_width = model_gain.shape[0]
    columns = stream_in.shape[1]
    capacity = 5 * tokens_here // (2 * expert_count)
    w_cols = lax.all_gather(out_weight, "ctx", axis=0, tiled=True)
    query3 = query_act.reshape(tokens_here, head_count, head_size)
    key3 = key_act.reshape(tokens_here, head_count, head_size)
    value3 = value_act.reshape(tokens_here, head_count, head_size)
    kv_own = jnp.einsum("thd,the->hde", key3, value3, preferred_element_type=f32)
    before, _ = butterfly_sums(kv_own, "ctx", False)
    prefix = state_init + before
    causal = jnp.arange(tokens_here)[:, None] >= jnp.arange(tokens_here)[None, :]
    scores = jnp.einsum("thd,shd->hts", query3, key3, preferred_element_type=f32)
    scores_bf = jnp.where(causal[None], scores, 0.0).astype(jnp.bfloat16)
    inside = jnp.einsum("hts,she->the", scores_bf, value3, preferred_element_type=f32)
    from_state = jnp.einsum("thd,hde->the", query3.astype(f32), prefix, precision=high)
    attended = from_state + inside
    gain_heads = head_gain.reshape(head_count, head_size)
    normed_heads = (
        head_normalize(attended, gain_heads)
        .astype(jnp.bfloat16)
        .reshape(tokens_here, head_count * head_size)
    )
    w_blocks = w_cols.reshape(ep_count, head_count * head_size, columns)
    attn_proj = jnp.einsum(
        "ith,ihf->tf", gather_blocks(normed_heads, "ep"), w_blocks, preferred_element_type=f32
    )
    stream = (stream_in.astype(f32) + attn_proj).astype(jnp.bfloat16)
    stream_f = stream.astype(f32)
    gain_cols = lax.dynamic_slice_in_dim(model_gain, my_ep * columns, columns, 0)
    dest_expert = jnp.arange(ep_count) % expert_count
    slot_iota = jnp.arange(capacity)
    hits = (expert_ids[:, :, None, None] == dest_expert[None, None, :, None]) & (
        expert_slots[:, :, None, None] == slot_iota[None, None, None, :]
    )
    hits_f = hits.astype(f32)
    dest_picks = jnp.sum(hits_f, 1).reshape(tokens_here, ep_count * capacity)
    dest_weights = jnp.sum(hits_f * route_gates[:, :, None, None], 1).reshape(
        tokens_here, ep_count * capacity
    )
    picked = jnp.dot(
        dest_picks.T.astype(jnp.bfloat16), stream, preferred_element_type=f32
    ).astype(jnp.bfloat16)
    arrived = lax.all_to_all(
        picked.reshape(ep_count, capacity, columns), "ep", 0, 0, tiled=True
    )
    slot_rows = arrived.transpose(1, 0, 2).reshape(capacity, model_width).astype(f32)
    slot_scale = lax.rsqrt(jnp.mean(slot_rows * slot_rows, -1, keepdims=True) + 1e-05)
    expert_in = (slot_rows * slot_scale * model_gain).astype(jnp.bfloat16)
    w_gate = gate_weight[0]
    w_up = up_weight[0]
    w_down = down_weight[0]
    hidden_block = w_gate.shape[0]
    w_rows = lax.all_to_all(w_blocks, "ep", 0, 0, tiled=True)
    portion = lax.all_gather(expert_in, "ctx", axis=0, tiled=True)
    square_sums = jnp.sum(gather_blocks(jnp.sum(stream_f * stream_f, -1, keepdims=True), "ep"), 0)
    portion, w_rows, square_sums = lax.optimization_barrier((portion, w_rows, square_sums))
    row_scale = lax.rsqrt(square_sums / model_width + 1e-05)
    projected = jnp.concatenate([contract_last(portion, w_gate), contract_last(portion, w_up)], 1)
    pre_gate = projected[:, :hidden_block]
    pre_up = projected[:, hidden_block:]
    gate_sig = jax.nn.sigmoid(pre_gate)
    activated = (pre_gate * gate_sig * pre_up).astype(jnp.bfloat16)
    out_terms = jnp.dot(activated, w_down, preferred_element_type=f32).astype(jnp.bfloat16)
    grad_out = out_grad.astype(f32)
    grad_send = jnp.dot(dest_weights.T, grad_out, precision=high).astype(jnp.bfloat16)
    grad_in = lax.all_to_all(grad_send, "ep", split_axis=0, concat_axis=1, tiled=True)
    grad_act = contract_last(lax.all_gather(grad_in, "ctx", axis=0, tiled=True), w_down)
    grad_gate_pre = (grad_act * pre_up * gate_sig * (1.0 + pre_gate * (1.0 - gate_sig))).astype(
        jnp.bfloat16
    )
    grad_up_pre = (grad_act * pre_gate * gate_sig).astype(jnp.bfloat16)
    grad_terms = (
        jnp.dot(grad_gate_pre, w_gate, preferred_element_type=f32)
        + jnp.dot(grad_up_pre, w_up, preferred_element_type=f32)
    ).astype(jnp.bfloat16)
    half_out, grad_half = scatter_sum([out_terms, grad_terms], "ctx")
    slot_inner = jnp.sum(slot_rows * model_gain * grad_half.astype(f32), -1, keepdims=True)
    inner_hi = slot_inner.astype(jnp.bfloat16)
    inner_lo = (slot_inner - inner_hi.astype(f32)).astype(jnp.bfloat16)
    inner_pair = jnp.broadcast_to(
        jnp.concatenate([inner_hi, inner_lo], -1)[:, None, :], (capacity, ep_count, 2)
    )
    payload = jnp.concatenate([grad_half.reshape(capacity, ep_count, columns), inner_pair], -1)
    grad_back = lax.all_to_all(payload, "ep", split_axis=1, concat_axis=0, tiled=True)
    grad_back = grad_back.reshape(ep_count * capacity, columns + 2).astype(f32)
    grad_model_in = jnp.dot(dest_picks, grad_back[:, :columns], precision=high)
    scaled_grad = grad_model_in * gain_cols
    inner_sum = jnp.dot(
        dest_picks, grad_back[:, columns:columns + 1] + grad_back[:, columns + 1:], precision=high
    )
    grad_stream = (
        grad_out
        + row_scale * scaled_grad
        - stream_f * row_scale**3 * inner_sum / model_width
    ).astype(jnp.bfloat16)
    grad_heads = jnp.einsum(
        "itf,ihf->th", gather_blocks(grad_stream, "ep"), w_rows, preferred_element_type=f32
    )
    head_pull = jax.vjp(lambda value: head_normalize(value, gain_heads), attended)[1]
    grad_attended = head_pull(grad_heads.reshape(tokens_here, head_count, head_size))[0].astype(
        jnp.bfloat16
    )
    state_part = jnp.einsum("thd,the->hde", query3, grad_attended, preferred_element_type=f32)
    half_out, state_part = lax.optimization_barrier((half_out, state_part))
    returned = lax.all_to_all(half_out, "ep", split_axis=1, concat_axis=0, tiled=True)
    expert_mix = jnp.dot(dest_weights, returned.astype(f32), precision=high)
    layer_out = (stream_f + expert_mix).astype(jnp.bfloat16)
    later_sum, state_total = butterfly_sums(state_part, "ctx", True)
    grad_scores = jnp.einsum("the,she->hts", grad_attended, value3, preferred_element_type=f32)
    grad_masked = jnp.where(causal[None], grad_scores, 0.0).astype(jnp.bfloat16)
    grad_att_f = grad_attended.astype(f32)
    grad_query = jnp.einsum("the,hde->thd", grad_att_f, prefix, precision=high) + jnp.einsum(
        "hts,shd->thd", grad_masked, key3, preferred_element_type=f32
    )
    grad_key = jnp.einsum(
        "the,hde->thd", value3.astype(f32), later_sum, precision=high
    ) + jnp.einsum("hts,thd->shd", grad_masked, query3, preferred_element_type=f32)
    grad_value = jnp.einsum(
        "thd,hde->the", key3.astype(f32), later_sum, precision=high
    ) + jnp.einsum("hts,the->she", scores_bf, grad_attended, preferred_element_type=f32)
    flat_shape = (tokens_here, head_count * head_size)
    return (
        layer_out,
        grad_query.astype(jnp.bfloat16).reshape(flat_shape),
        grad_key.astype(jnp.bfloat16).reshape(flat_shape),
        grad_value.astype(jnp.bfloat16).reshape(flat_shape),
        state_total,
        grad_stream,
    )


def solution(mesh):
    return jax.shard_map(
        local,
        mesh=mesh,
        in_specs=(
            P("ctx", "ep"),
            P("ctx", "ep"),
            P("ctx", "ep"),
            P("ep", None, None),
            P("ep"),
            P("ctx", "ep"),
            P("ctx", "ep"),
            P(),
            P("ctx", None),
            P("ctx", None),
            P("ctx", None),
            P("ep", "ctx", None),
            P("ep", "ctx", None),
            P("ep", "ctx", None),
            P("ctx", "ep"),
        ),
        out_specs=(
            P("ctx", "ep"),
            P("ctx", "ep"),
            P("ctx", "ep"),
            P("ctx", "ep"),
            P("ep", None, None),
            P("ctx", "ep"),
        ),
        check_vma=False,
    )
```

```python
import jax
import jax.numpy as jnp
from jax import lax
from jax.sharding import PartitionSpec as P


def butterfly_sums(value, axis, backward):
    count = lax.axis_size(axis)
    place = lax.axis_index(axis)
    total = value
    carried = jnp.zeros_like(value)
    step = 1
    while step < count:
        other = lax.ppermute(total, axis, [(i, i ^ step) for i in range(count)])
        upper = (place & step) != 0
        take = jnp.logical_not(upper) if backward else upper
        carried = carried + jnp.where(take, other, jnp.zeros_like(other))
        total = total + other
        step *= 2
    return carried, total


def gather_blocks(value, axis):
    count = lax.axis_size(axis)
    spread = jnp.broadcast_to(value[None], (count,) + value.shape)
    return lax.all_to_all(spread, axis, 0, 0, tiled=True)


def scatter_sum(values, axis):
    count = lax.axis_size(axis)
    rows, width = values[0].shape
    block = rows // count
    joined = jnp.concatenate([value.reshape(count, block, width) for value in values], 1)
    part = lax.psum_scatter(joined, axis, scatter_dimension=0, tiled=True)
    return [part[0, i * block:(i + 1) * block] for i in range(len(values))]


def head_normalize(attended, gain):
    factor = lax.rsqrt(jnp.mean(attended * attended, -1, keepdims=True) + 1e-06)
    return attended * factor * gain


def contract_last(left, right):
    return lax.dot_general(
        left, right, (((1,), (1,)), ((), ())), preferred_element_type=jnp.float32
    )


def local(
    query_act,
    key_act,
    value_act,
    state_init,
    head_gain,
    out_weight,
    stream_in,
    model_gain,
    expert_ids,
    expert_slots,
    route_gates,
    gate_weight,
    up_weight,
    down_weight,
    out_grad,
):
    f32 = jnp.float32
    high = lax.Precision.HIGHEST
    ep_count = lax.axis_size("ep")
    expert_count = ep_count // 2
    my_ep = lax.axis_index("ep")
    tokens_here = query_act.shape[0]
    head_count = state_init.shape[0]
    head_size = state_init.shape[1]
    model_width = model_gain.shape[0]
    columns = stream_in.shape[1]
    capacity = 5 * tokens_here // (2 * expert_count)
    w_cols = lax.all_gather(out_weight, "ctx", axis=0, tiled=True)
    query3 = query_act.reshape(tokens_here, head_count, head_size)
    key3 = key_act.reshape(tokens_here, head_count, head_size)
    value3 = value_act.reshape(tokens_here, head_count, head_size)
    kv_own = jnp.einsum("thd,the->hde", key3, value3, preferred_element_type=f32)
    before, _ = butterfly_sums(kv_own, "ctx", False)
    prefix = state_init + before
    causal = jnp.arange(tokens_here)[:, None] >= jnp.arange(tokens_here)[None, :]
    scores = jnp.einsum("thd,shd->hts", query3, key3, preferred_element_type=f32)
    scores_bf = jnp.where(causal[None], scores, 0.0).astype(jnp.bfloat16)
    inside = jnp.einsum("hts,she->the", scores_bf, value3, preferred_element_type=f32)
    from_state = jnp.einsum("thd,hde->the", query3.astype(f32), prefix, precision=high)
    attended = from_state + inside
    gain_heads = head_gain.reshape(head_count, head_size)
    normed_heads = (
        head_normalize(attended, gain_heads)
        .astype(jnp.bfloat16)
        .reshape(tokens_here, head_count * head_size)
    )
    w_blocks = w_cols.reshape(ep_count, head_count * head_size, columns)
    attn_proj = jnp.einsum(
        "ith,ihf->tf", gather_blocks(normed_heads, "ep"), w_blocks, preferred_element_type=f32
    )
    stream = (stream_in.astype(f32) + attn_proj).astype(jnp.bfloat16)
    stream_f = stream.astype(f32)
    gain_cols = lax.dynamic_slice_in_dim(model_gain, my_ep * columns, columns, 0)
    dest_expert = jnp.arange(ep_count) % expert_count
    slot_iota = jnp.arange(capacity)
    hits = (expert_ids[:, :, None, None] == dest_expert[None, None, :, None]) & (
        expert_slots[:, :, None, None] == slot_iota[None, None, None, :]
    )
    hits_f = hits.astype(f32)
    dest_picks = jnp.sum(hits_f, 1).reshape(tokens_here, ep_count * capacity)
    dest_weights = jnp.sum(hits_f * route_gates[:, :, None, None], 1).reshape(
        tokens_here, ep_count * capacity
    )
    picked = jnp.dot(
        dest_picks.T.astype(jnp.bfloat16), stream, preferred_element_type=f32
    ).astype(jnp.bfloat16)
    arrived = lax.all_to_all(
        picked.reshape(ep_count, capacity, columns), "ep", 0, 0, tiled=True
    )
    slot_rows = arrived.transpose(1, 0, 2).reshape(capacity, model_width).astype(f32)
    slot_scale = lax.rsqrt(jnp.mean(slot_rows * slot_rows, -1, keepdims=True) + 1e-05)
    expert_in = (slot_rows * slot_scale * model_gain).astype(jnp.bfloat16)
    w_gate = gate_weight[0]
    w_up = up_weight[0]
    w_down = down_weight[0]
    hidden_block = w_gate.shape[0]
    w_rows = lax.all_to_all(w_blocks, "ep", 0, 0, tiled=True)
    portion = lax.all_gather(expert_in, "ctx", axis=0, tiled=True)
    square_sums = jnp.sum(gather_blocks(jnp.sum(stream_f * stream_f, -1, keepdims=True), "ep"), 0)
    row_scale = lax.rsqrt(square_sums / model_width + 1e-05)
    projected = jnp.concatenate([contract_last(portion, w_gate), contract_last(portion, w_up)], 1)
    pre_gate = projected[:, :hidden_block]
    pre_up = projected[:, hidden_block:]
    gate_sig = jax.nn.sigmoid(pre_gate)
    activated = (pre_gate * gate_sig * pre_up).astype(jnp.bfloat16)
    out_terms = jnp.dot(activated, w_down, preferred_element_type=f32).astype(jnp.bfloat16)
    grad_out = out_grad.astype(f32)
    grad_send = jnp.dot(dest_weights.T, grad_out, precision=high).astype(jnp.bfloat16)
    grad_in = lax.all_to_all(grad_send, "ep", split_axis=0, concat_axis=1, tiled=True)
    grad_rows_all = lax.all_gather(grad_in, "ctx", axis=0, tiled=True)
    portion, w_rows, square_sums, grad_rows_all = lax.optimization_barrier(
        (portion, w_rows, square_sums, grad_rows_all)
    )
    row_scale = lax.rsqrt(square_sums / model_width + 1e-05)
    grad_act = contract_last(grad_rows_all, w_down)
    grad_gate_pre = (grad_act * pre_up * gate_sig * (1.0 + pre_gate * (1.0 - gate_sig))).astype(
        jnp.bfloat16
    )
    grad_up_pre = (grad_act * pre_gate * gate_sig).astype(jnp.bfloat16)
    grad_terms = (
        jnp.dot(grad_gate_pre, w_gate, preferred_element_type=f32)
        + jnp.dot(grad_up_pre, w_up, preferred_element_type=f32)
    ).astype(jnp.bfloat16)
    half_out, grad_half = scatter_sum([out_terms, grad_terms], "ctx")
    slot_inner = jnp.sum(slot_rows * model_gain * grad_half.astype(f32), -1, keepdims=True)
    inner_hi = slot_inner.astype(jnp.bfloat16)
    inner_lo = (slot_inner - inner_hi.astype(f32)).astype(jnp.bfloat16)
    inner_pair = jnp.broadcast_to(
        jnp.concatenate([inner_hi, inner_lo], -1)[:, None, :], (capacity, ep_count, 2)
    )
    payload = jnp.concatenate([grad_half.reshape(capacity, ep_count, columns), inner_pair], -1)
    grad_back = lax.all_to_all(payload, "ep", split_axis=1, concat_axis=0, tiled=True)
    grad_back = grad_back.reshape(ep_count * capacity, columns + 2).astype(f32)
    grad_model_in = jnp.dot(dest_picks, grad_back[:, :columns], precision=high)
    scaled_grad = grad_model_in * gain_cols
    inner_sum = jnp.dot(
        dest_picks, grad_back[:, columns:columns + 1] + grad_back[:, columns + 1:], precision=high
    )
    grad_stream = (
        grad_out
        + row_scale * scaled_grad
        - stream_f * row_scale**3 * inner_sum / model_width
    ).astype(jnp.bfloat16)
    grad_heads = jnp.einsum(
        "itf,ihf->th", gather_blocks(grad_stream, "ep"), w_rows, preferred_element_type=f32
    )
    head_pull = jax.vjp(lambda value: head_normalize(value, gain_heads), attended)[1]
    grad_attended = head_pull(grad_heads.reshape(tokens_here, head_count, head_size))[0].astype(
        jnp.bfloat16
    )
    state_part = jnp.einsum("thd,the->hde", query3, grad_attended, preferred_element_type=f32)
    half_out, state_part = lax.optimization_barrier((half_out, state_part))
    returned = lax.all_to_all(half_out, "ep", split_axis=1, concat_axis=0, tiled=True)
    expert_mix = jnp.dot(dest_weights, returned.astype(f32), precision=high)
    layer_out = (stream_f + expert_mix).astype(jnp.bfloat16)
    later_sum, state_total = butterfly_sums(state_part, "ctx", True)
    grad_scores = jnp.einsum("the,she->hts", grad_attended, value3, preferred_element_type=f32)
    grad_masked = jnp.where(causal[None], grad_scores, 0.0).astype(jnp.bfloat16)
    grad_att_f = grad_attended.astype(f32)
    grad_query = jnp.einsum("the,hde->thd", grad_att_f, prefix, precision=high) + jnp.einsum(
        "hts,shd->thd", grad_masked, key3, preferred_element_type=f32
    )
    grad_key = jnp.einsum(
        "the,hde->thd", value3.astype(f32), later_sum, precision=high
    ) + jnp.einsum("hts,thd->shd", grad_masked, query3, preferred_element_type=f32)
    grad_value = jnp.einsum(
        "thd,hde->the", key3.astype(f32), later_sum, precision=high
    ) + jnp.einsum("hts,the->she", scores_bf, grad_attended, preferred_element_type=f32)
    flat_shape = (tokens_here, head_count * head_size)
    return (
        layer_out,
        grad_query.astype(jnp.bfloat16).reshape(flat_shape),
        grad_key.astype(jnp.bfloat16).reshape(flat_shape),
        grad_value.astype(jnp.bfloat16).reshape(flat_shape),
        state_total,
        grad_stream,
    )


def solution(mesh):
    return jax.shard_map(
        local,
        mesh=mesh,
        in_specs=(
            P("ctx", "ep"),
            P("ctx", "ep"),
            P("ctx", "ep"),
            P("ep", None, None),
            P("ep"),
            P("ctx", "ep"),
            P("ctx", "ep"),
            P(),
            P("ctx", None),
            P("ctx", None),
            P("ctx", None),
            P("ep", "ctx", None),
            P("ep", "ctx", None),
            P("ep", "ctx", None),
            P("ctx", "ep"),
        ),
        out_specs=(
            P("ctx", "ep"),
            P("ctx", "ep"),
            P("ctx", "ep"),
            P("ctx", "ep"),
            P("ep", None, None),
            P("ctx", "ep"),
        ),
        check_vma=False,
    )
```
